32 devices in a mesh: lang: 4 (over x, core), dp: 8 (over z, y).
Axes of the slice: x: 2, y: 2, z: 4, core: 2. Of those that a mesh axis runs over, the one named last changes fastest.
Arguments:
- src_emb: bfloat16 [4096, 768], P(('lang', 'dp')), may hold values from -6 to 6
- tgt_emb: bfloat16 [4, 1024, 768], P(None, ('lang', 'dp')), may hold values from -6 to 6
- slot_group: int32 [4], replicated, may hold values from 0 to 3, each once
- counts: int32 [4], replicated, may hold values from 256 to 1024, as said below
- align: int32 [4, 1024], P('lang'), may hold values from 0 to 1023, each once within a row
- pair_weight: float32 [4], replicated, may hold values from 4 to 40
Outputs:
- grad_src: bfloat16 [4096, 768], P(('lang', 'dp'))
- grad_tgt: bfloat16 [4, 1024, 768], P(None, ('lang', 'dp'))
- pair_loss: float32 [4], P('lang')
The draws below stay inside these ranges and needn't reach their ends.
Inputs may be any that keep to these rules, and one draw needn't show every extreme that they name: `counts`: at least one pair has all 1024 sentences live. `align`: each row is a permutation.
All inputs are finite; a program needn't handle non-finite values.
Results may differ from the reference program's by a relative error of at most 0.0057.
Values may be sent and summed in bfloat16 or wider, within the bound.
No kernel may reach another device: no remote copies, remote signals or barrier semaphores. Data moves between devices by JAX's collectives and lax.ppermute only.
A program may use at most 64 MiB of HBM per device.

```python
import math
import jax
import jax.numpy as jnp
from jax import lax

D = 768
LANGS = 4
PAIR_ROWS = 1024
TOTAL = 4096


def shared_vector(key, salt):
    signs = jnp.where(jax.random.bernoulli(jax.random.fold_in(key, salt), 0.5, (D,)), 1.0, -1.0)
    sizes = jax.random.uniform(jax.random.fold_in(key, salt + 1), (D,), jnp.float32, 4.9, 5.1)
    return signs * sizes


def draw_src_emb(key, part):
    base = jax.random.normal(key, (TOTAL, D), jnp.float32)
    within = jnp.arange(TOTAL) % PAIR_ROWS
    first_vec = shared_vector(key, 7)
    second_vec = shared_vector(key, 9)
    spike_row = (within < 4)[:, None]
    spike_vec = jnp.where((within < 2)[:, None], first_vec[None, :], second_vec[None, :])
    factor = jnp.where(within % 2 == 0, 1.0, 0.95)[:, None]
    values = jnp.where(spike_row, factor * spike_vec, base)
    return jnp.clip(values, -6.0, 6.0).astype(jnp.bfloat16)


def draw_tgt_emb(key, part):
    base = jax.random.normal(jax.random.fold_in(key, 11), (LANGS, PAIR_ROWS, D), jnp.float32)
    strength = jax.random.uniform(jax.random.fold_in(key, 14), (LANGS, PAIR_ROWS, 1), jnp.float32, 0.3, 1.0)
    index = jnp.arange(PAIR_ROWS)
    first_vec = shared_vector(key, 7)
    second_vec = shared_vector(key, 9)
    which_vec = jnp.where((index % 128 == 0)[:, None], first_vec[None, :], second_vec[None, :])
    spike_row = (index % 64 == 0)[None, :, None]
    values = jnp.where(spike_row, strength * which_vec[None, :, :], base)
    return jnp.clip(values, -6.0, 6.0).astype(jnp.bfloat16)


def draw_counts(key, part):
    raw_counts = jax.random.randint(jax.random.fold_in(key, 21), (LANGS,), PAIR_ROWS // 4, PAIR_ROWS + 1)
    chosen = jax.random.randint(jax.random.fold_in(key, 22), (), 0, LANGS)
    return jnp.where(jnp.arange(LANGS) == chosen, PAIR_ROWS, raw_counts).astype(jnp.int32)


def setup_inputs(seed: int = 0) -> dict:
    seeds = jax.random.split(jax.random.key(seed), 7)
    return {
        "src_emb": draw_src_emb(jax.random.fold_in(seeds[6], 71), 0),
        "tgt_emb": draw_tgt_emb(jax.random.fold_in(seeds[6], 71), 0),
        "slot_group": jax.random.permutation(seeds[2], LANGS).astype(jnp.int32),
        "counts": draw_counts(jax.random.fold_in(seeds[6], 71), 0),
        "align": jax.vmap(lambda own: jax.random.permutation(own, PAIR_ROWS))(jax.random.split(seeds[4], LANGS)).reshape((LANGS, PAIR_ROWS)).astype(jnp.int32),
        "pair_weight": jnp.clip(jnp.exp(jax.random.uniform(seeds[5], (LANGS,), jnp.float32, math.log(4.0), math.log(40.0))), 4.0, 40.0),
    }


MARGIN = 0.3
LOW_FILL = -1e+30

def reference(src_emb, tgt_emb, slot_group, counts, align, pair_weight):
    inv_root = 1.0 / math.sqrt(D)
    slot_ids = jnp.arange(LANGS, dtype=jnp.int32)
    slot_of_group = jnp.zeros((LANGS,), jnp.int32).at[slot_group].set(slot_ids)
    sources = src_emb.reshape(LANGS, PAIR_ROWS, D)
    targets = tgt_emb[slot_of_group]

    def one_pair(pair_items):
        src_rows, tgt_rows, link_index, live_count, weight = pair_items
        all_rows = jnp.arange(PAIR_ROWS, dtype=jnp.int32)
        row_live = all_rows < live_count
        col_live = jnp.zeros((PAIR_ROWS,), jnp.int32).at[link_index].set(row_live.astype(jnp.int32)) > 0
        is_pos = all_rows[None, :] == link_index[:, None]
        scores_f = jnp.dot(src_rows, tgt_rows.T, preferred_element_type=jnp.float32) * inv_root
        scores_f = scores_f - MARGIN * is_pos.astype(jnp.float32)
        row_max = lax.optimization_barrier(jnp.max(jnp.where(col_live[None, :], scores_f, LOW_FILL), axis=1))
        row_sum = lax.optimization_barrier(jnp.sum(jnp.where(col_live[None, :], jnp.exp(scores_f - row_max[:, None]), 0.0), axis=1))
        row_lse = row_max + jnp.log(row_sum + (1.0 - row_live.astype(jnp.float32)))
        col_max = lax.optimization_barrier(jnp.max(jnp.where(row_live[:, None], scores_f, LOW_FILL), axis=0))
        col_sum = lax.optimization_barrier(jnp.sum(jnp.where(row_live[:, None], jnp.exp(scores_f - col_max[None, :]), 0.0), axis=0))
        col_lse = col_max + jnp.log(col_sum + (1.0 - col_live.astype(jnp.float32)))
        pos_score = lax.optimization_barrier(jnp.sum(jnp.where(is_pos, scores_f, 0.0), axis=1))
        terms = jnp.where(row_live, row_lse + col_lse[link_index] - 2.0 * pos_score, 0.0)
        loss_value = jnp.sum(terms) / live_count.astype(jnp.float32)
        both_live = row_live[:, None] & col_live[None, :]
        by_row = jnp.where(both_live, jnp.exp(scores_f - row_lse[:, None]), 0.0)
        by_col = jnp.where(both_live, jnp.exp(scores_f - col_lse[None, :]), 0.0)
        pos_hit = (is_pos & row_live[:, None]).astype(jnp.float32)
        grad_tile = (weight * (by_row + by_col - 2.0 * pos_hit)).astype(jnp.bfloat16)
        grad_rows = jnp.dot(grad_tile, tgt_rows, preferred_element_type=jnp.float32) * inv_root
        grad_cols = jnp.dot(grad_tile.T, src_rows, preferred_element_type=jnp.float32) * inv_root
        return (grad_rows.astype(jnp.bfloat16), grad_cols.astype(jnp.bfloat16), loss_value)
    grad_rows, grad_cols, pair_loss = lax.map(one_pair, (sources, targets, align, counts, pair_weight))
    grad_src = grad_rows.reshape(TOTAL, D)
    grad_tgt = grad_cols[slot_group]
    return (grad_src, grad_tgt, pair_loss)
```

```python
import math

import jax
import jax.numpy as jnp
from jax import lax
from jax.sharding import PartitionSpec as P

MARGIN = 0.3
LOW_FILL = -1e30
BLOCK_BYTES = 8 * 1024 * 1024


def target_index(col_count, row_count, per_slot, data_size):
    position = jnp.arange(col_count, dtype=jnp.int32)
    source = position // row_count
    within = position % row_count
    return (within // per_slot * data_size + source) * per_slot + within % per_slot


def scores_of(x_rows, y_rows, pos_mask, inv_root):
    raw_dot = lax.dot_general(
        x_rows, y_rows, (((1,), (1,)), ((), ())), preferred_element_type=jnp.float32
    )
    return raw_dot * inv_root - MARGIN * pos_mask.astype(jnp.float32)


def block_stats(scores_f, is_pos, row_live, col_ok):
    row_max = jnp.max(jnp.where(col_ok[None, :], scores_f, LOW_FILL), axis=1)
    row_sum = jnp.sum(
        jnp.where(col_ok[None, :], jnp.exp(scores_f - row_max[:, None]), 0.0), axis=1
    )
    row_lse = row_max + jnp.log(row_sum + (1.0 - row_live.astype(jnp.float32)))
    pos_score = jnp.sum(jnp.where(is_pos, scores_f, 0.0), axis=1)
    col_max = jnp.max(jnp.where(row_live[:, None], scores_f, LOW_FILL), axis=0)
    col_sum = jnp.sum(
        jnp.where(row_live[:, None], jnp.exp(scores_f - col_max[None, :]), 0.0), axis=0
    )
    return row_lse, pos_score, col_max, col_sum


def grad_of(scores_f, is_pos, row_ok, col_ok, row_lse, col_lse, weight):
    both_live = row_ok[:, None] & col_ok[None, :]
    by_row = jnp.where(both_live, jnp.exp(scores_f - row_lse[:, None]), 0.0)
    by_col = jnp.where(both_live, jnp.exp(scores_f - col_lse[None, :]), 0.0)
    pos_hit = (is_pos & row_ok[:, None]).astype(jnp.float32)
    return (weight * (by_row + by_col - 2.0 * pos_hit)).astype(jnp.bfloat16)


def per_device(src_emb, tgt_emb, slot_group, counts, align, pair_weight):
    lang_size = lax.axis_size("lang")
    data_size = lax.axis_size("dp")
    row_count, emb_width = src_emb.shape
    per_slot = tgt_emb.shape[1]
    pair_rows = row_count * data_size
    inv_root = 1.0 / math.sqrt(emb_width)
    group_index = lax.axis_index("lang")
    shard_index = lax.axis_index("dp")
    slot_ids = jnp.arange(lang_size, dtype=jnp.int32)
    slot_of_group = jnp.zeros((lang_size,), jnp.int32).at[slot_group].set(slot_ids)
    ordered = tgt_emb[slot_of_group]
    arrived = lax.all_to_all(ordered, "lang", split_axis=0, concat_axis=1, tiled=True)
    partner = arrived[0]
    live_count = counts[group_index]
    weight = pair_weight[group_index]
    pair_align = align[0]
    all_rows = jnp.arange(pair_rows, dtype=jnp.int32)
    row_live = all_rows < live_count
    col_live_global = (
        jnp.zeros((pair_rows,), jnp.int32).at[pair_align].set(row_live.astype(jnp.int32))
    )
    perm = target_index(pair_rows, row_count, per_slot, data_size)
    col_live = col_live_global[perm] > 0
    x_all = lax.all_gather(src_emb, "dp", axis=0, tiled=True)
    y_all = lax.all_gather(partner, "dp", axis=0, tiled=True)

    block = max(1, min(pair_rows, BLOCK_BYTES // (4 * pair_rows)))
    steps = pair_rows // block
    if steps == 1:
        is_pos = perm[None, :] == pair_align[:, None]
        scores_f = scores_of(x_all, y_all, is_pos, inv_root)
        row_lse, pos_score, col_max, col_sum = block_stats(scores_f, is_pos, row_live, col_live)
    else:
        def one_block(k, carry):
            row_lse, pos_score, col_max, col_sum = carry
            start = k * block
            x_blk = lax.dynamic_slice_in_dim(x_all, start, block)
            a_blk = lax.dynamic_slice_in_dim(pair_align, start, block)
            r_blk = lax.dynamic_slice_in_dim(row_live, start, block)
            is_pos = perm[None, :] == a_blk[:, None]
            s_blk = scores_of(x_blk, y_all, is_pos, inv_root)
            b_lse, b_pos, b_max, b_sum = block_stats(s_blk, is_pos, r_blk, col_live)
            top = jnp.maximum(col_max, b_max)
            col_sum = col_sum * jnp.exp(col_max - top) + b_sum * jnp.exp(b_max - top)
            row_lse = lax.dynamic_update_slice_in_dim(row_lse, b_lse, start, 0)
            pos_score = lax.dynamic_update_slice_in_dim(pos_score, b_pos, start, 0)
            return row_lse, pos_score, top, col_sum

        zeros = jnp.zeros((pair_rows,), jnp.float32)
        init = (zeros, zeros, jnp.full((pair_rows,), LOW_FILL, jnp.float32), zeros)
        row_lse, pos_score, col_max, col_sum = lax.fori_loop(0, steps, one_block, init)
    col_lse = col_max + jnp.log(col_sum + (1.0 - col_live.astype(jnp.float32)))

    row_f = row_live.astype(jnp.float32)
    col_f = col_live.astype(jnp.float32)
    total = jnp.sum(row_f * (row_lse - 2.0 * pos_score)) + jnp.sum(col_f * col_lse)
    pair_loss = (total / live_count.astype(jnp.float32)).reshape(1)

    mine = shard_index * row_count
    x_my = lax.dynamic_slice_in_dim(x_all, mine, row_count)
    a_my = lax.dynamic_slice_in_dim(pair_align, mine, row_count)
    r_my = lax.dynamic_slice_in_dim(row_live, mine, row_count)
    lse_my = lax.dynamic_slice_in_dim(row_lse, mine, row_count)
    pos_rows = perm[None, :] == a_my[:, None]
    s_rows = scores_of(x_my, y_all, pos_rows, inv_root)
    g_rows = grad_of(s_rows, pos_rows, r_my, col_live, lse_my, col_lse, weight)
    grad_src = (
        jnp.dot(g_rows, y_all, preferred_element_type=jnp.float32) * inv_root
    ).astype(jnp.bfloat16)

    p_my = lax.dynamic_slice_in_dim(perm, mine, row_count)
    c_my = lax.dynamic_slice_in_dim(col_live, mine, row_count)
    clse_my = lax.dynamic_slice_in_dim(col_lse, mine, row_count)
    pos_cols = p_my[None, :] == pair_align[:, None]
    s_cols = scores_of(x_all, partner, pos_cols, inv_root)
    g_cols = grad_of(s_cols, pos_cols, row_live, c_my, row_lse, clse_my, weight)
    own_terms = lax.dot_general(
        g_cols, x_all, (((0,), (0,)), ((), ())), preferred_element_type=jnp.float32
    )
    grad_local = (own_terms * inv_root).astype(jnp.bfloat16)
    returned = lax.all_to_all(
        grad_local.reshape(1, row_count, emb_width), "lang", split_axis=1, concat_axis=0, tiled=True
    )
    grad_tgt = returned[slot_group]
    return (grad_src, grad_tgt, pair_loss)


def solution(mesh):
    in_specs = (
        P(("lang", "dp"), None),
        P(None, ("lang", "dp"), None),
        P(),
        P(),
        P("lang", None),
        P(),
    )
    out_specs = (P(("lang", "dp"), None), P(None, ("lang", "dp"), None), P("lang"))
    return jax.shard_map(
        per_device, mesh=mesh, in_specs=in_specs, out_specs=out_specs, check_vma=False
    )
```

```python
import functools
import math

import jax
import jax.numpy as jnp
from jax import lax
from jax.sharding import PartitionSpec as P

MARGIN = 0.3
LOW_FILL = -1e30
BLOCK_BYTES = 8 * 1024 * 1024


def target_index(col_count, row_count, per_slot, data_size):
    position = jnp.arange(col_count, dtype=jnp.int32)
    source = position // row_count
    within = position % row_count
    return (within // per_slot * data_size + source) * per_slot + within % per_slot


def snake_ring(mesh):
    count = mesh.shape["dp"]
    try:
        spots = [tuple(dev.coords) for dev in mesh.devices.reshape(-1, count)[0]]
    except (AttributeError, TypeError):
        return list(range(count))
    ys = sorted({s[1] for s in spots})
    zs = sorted({s[2] for s in spots})
    where = {(s[1], s[2]): d for d, s in enumerate(spots)}
    if len(where) != count or len(ys) * len(zs) != count:
        return list(range(count))
    rows, cols = (ys, zs) if len(ys) % 2 == 0 else (zs, ys)
    at = lambda r, c: where[(r, c) if rows is ys else (c, r)]
    if len(rows) == 1 or len(cols) == 1:
        return [at(r, c) for r in rows for c in cols]
    order = [at(rows[0], cols[0])]
    for k, r in enumerate(rows):
        seq = cols[1:] if k % 2 == 0 else cols[:0:-1]
        order += [at(r, c) for c in seq]
    order += [at(r, cols[0]) for r in rows[:0:-1]]
    return order


def ring_gather(block, ring):
    count = len(ring)
    place = [0] * count
    for p, d in enumerate(ring):
        place[d] = p
    ring_arr = jnp.array(ring, jnp.int32)
    my_dp = lax.axis_index("dp")
    my_pos = jnp.array(place, jnp.int32)[my_dp]
    ahead = [(ring[p], ring[(p + 1) % count]) for p in range(count)]
    behind = [(ring[p], ring[(p - 1) % count]) for p in range(count)]
    rows = block.shape[0]
    out = jnp.zeros((count * rows,) + block.shape[1:], block.dtype)
    out = lax.dynamic_update_slice_in_dim(out, block, my_dp * rows, 0)
    for pairs, steps, sign in ((ahead, count // 2, -1), (behind, count - 1 - count // 2, 1)):
        cur = block
        for t in range(1, steps + 1):
            cur = lax.ppermute(cur, "dp", pairs)
            origin = ring_arr[(my_pos + sign * t) % count]
            out = lax.dynamic_update_slice_in_dim(out, cur, origin * rows, 0)
    return out


def scores_of(x_rows, y_rows, pos_mask, inv_root):
    raw_dot = lax.dot_general(
        x_rows, y_rows, (((1,), (1,)), ((), ())), preferred_element_type=jnp.float32
    )
    return raw_dot * inv_root - MARGIN * pos_mask.astype(jnp.float32)


def block_stats(scores_f, is_pos, row_live, col_ok):
    row_max = jnp.max(jnp.where(col_ok[None, :], scores_f, LOW_FILL), axis=1)
    row_sum = jnp.sum(
        jnp.where(col_ok[None, :], jnp.exp(scores_f - row_max[:, None]), 0.0), axis=1
    )
    row_lse = row_max + jnp.log(row_sum + (1.0 - row_live.astype(jnp.float32)))
    pos_score = jnp.sum(jnp.where(is_pos, scores_f, 0.0), axis=1)
    col_max = jnp.max(jnp.where(row_live[:, None], scores_f, LOW_FILL), axis=0)
    col_sum = jnp.sum(
        jnp.where(row_live[:, None], jnp.exp(scores_f - col_max[None, :]), 0.0), axis=0
    )
    return row_lse, pos_score, col_max, col_sum


def grad_of(scores_f, is_pos, row_ok, col_ok, row_lse, col_lse, weight):
    both_live = row_ok[:, None] & col_ok[None, :]
    by_row = jnp.where(both_live, jnp.exp(scores_f - row_lse[:, None]), 0.0)
    by_col = jnp.where(both_live, jnp.exp(scores_f - col_lse[None, :]), 0.0)
    pos_hit = (is_pos & row_ok[:, None]).astype(jnp.float32)
    return (weight * (by_row + by_col - 2.0 * pos_hit)).astype(jnp.bfloat16)


def per_device(ring, src_emb, tgt_emb, slot_group, counts, align, pair_weight):
    lang_size = lax.axis_size("lang")
    data_size = lax.axis_size("dp")
    row_count, emb_width = src_emb.shape
    per_slot = tgt_emb.shape[1]
    pair_rows = row_count * data_size
    inv_root = 1.0 / math.sqrt(emb_width)
    group_index = lax.axis_index("lang")
    shard_index = lax.axis_index("dp")
    slot_ids = jnp.arange(lang_size, dtype=jnp.int32)
    slot_of_group = jnp.zeros((lang_size,), jnp.int32).at[slot_group].set(slot_ids)
    ordered = tgt_emb[slot_of_group]
    arrived = lax.all_to_all(ordered, "lang", split_axis=0, concat_axis=1, tiled=True)
    partner = arrived[0]
    live_count = counts[group_index]
    weight = pair_weight[group_index]
    pair_align = align[0]
    all_rows = jnp.arange(pair_rows, dtype=jnp.int32)
    row_live = all_rows < live_count
    perm = target_index(pair_rows, row_count, per_slot, data_size)
    live_pos = (perm[None, :] == pair_align[:, None]) & row_live[:, None]
    col_live = jnp.max(live_pos.astype(jnp.int32), axis=0) > 0
    x_all = ring_gather(src_emb, ring)
    y_all = ring_gather(partner, ring)

    block = max(1, min(pair_rows, BLOCK_BYTES // (4 * pair_rows)))
    steps = pair_rows // block
    if steps == 1:
        is_pos = perm[None, :] == pair_align[:, None]
        scores_f = scores_of(x_all, y_all, is_pos, inv_root)
        row_lse, pos_score, col_max, col_sum = block_stats(scores_f, is_pos, row_live, col_live)
    else:
        def one_block(k, carry):
            row_lse, pos_score, col_max, col_sum = carry
            start = k * block
            x_blk = lax.dynamic_slice_in_dim(x_all, start, block)
            a_blk = lax.dynamic_slice_in_dim(pair_align, start, block)
            r_blk = lax.dynamic_slice_in_dim(row_live, start, block)
            is_pos = perm[None, :] == a_blk[:, None]
            s_blk = scores_of(x_blk, y_all, is_pos, inv_root)
            b_lse, b_pos, b_max, b_sum = block_stats(s_blk, is_pos, r_blk, col_live)
            top = jnp.maximum(col_max, b_max)
            col_sum = col_sum * jnp.exp(col_max - top) + b_sum * jnp.exp(b_max - top)
            row_lse = lax.dynamic_update_slice_in_dim(row_lse, b_lse, start, 0)
            pos_score = lax.dynamic_update_slice_in_dim(pos_score, b_pos, start, 0)
            return row_lse, pos_score, top, col_sum

        zeros = jnp.zeros((pair_rows,), jnp.float32)
        init = (zeros, zeros, jnp.full((pair_rows,), LOW_FILL, jnp.float32), zeros)
        row_lse, pos_score, col_max, col_sum = lax.fori_loop(0, steps, one_block, init)
    col_lse = col_max + jnp.log(col_sum + (1.0 - col_live.astype(jnp.float32)))

    row_f = row_live.astype(jnp.float32)
    col_f = col_live.astype(jnp.float32)
    total = jnp.sum(row_f * (row_lse - 2.0 * pos_score)) + jnp.sum(col_f * col_lse)
    pair_loss = (total / live_count.astype(jnp.float32)).reshape(1)

    mine = shard_index * row_count
    a_my = lax.dynamic_slice_in_dim(pair_align, mine, row_count)
    r_my = lax.dynamic_slice_in_dim(row_live, mine, row_count)
    lse_my = lax.dynamic_slice_in_dim(row_lse, mine, row_count)
    pos_rows = perm[None, :] == a_my[:, None]
    s_rows = scores_of(src_emb, y_all, pos_rows, inv_root)
    g_rows = grad_of(s_rows, pos_rows, r_my, col_live, lse_my, col_lse, weight)
    grad_src = (
        jnp.dot(g_rows, y_all, preferred_element_type=jnp.float32) * inv_root
    ).astype(jnp.bfloat16)

    p_my = lax.dynamic_slice_in_dim(perm, mine, row_count)
    c_my = lax.dynamic_slice_in_dim(col_live, mine, row_count)
    clse_my = lax.dynamic_slice_in_dim(col_lse, mine, row_count)
    pos_cols = p_my[None, :] == pair_align[:, None]
    s_cols = scores_of(x_all, partner, pos_cols, inv_root)
    g_cols = grad_of(s_cols, pos_cols, row_live, c_my, row_lse, clse_my, weight)
    own_terms = lax.dot_general(
        g_cols, x_all, (((0,), (0,)), ((), ())), preferred_element_type=jnp.float32
    )
    grad_local = (own_terms * inv_root).astype(jnp.bfloat16)
    returned = lax.all_to_all(
        grad_local.reshape(1, row_count, emb_width), "lang", split_axis=1, concat_axis=0, tiled=True
    )
    grad_tgt = returned[slot_group]
    return (grad_src, grad_tgt, pair_loss)


def solution(mesh):
    in_specs = (
        P(("lang", "dp"), None),
        P(None, ("lang", "dp"), None),
        P(),
        P(),
        P("lang", None),
        P(),
    )
    out_specs = (P(("lang", "dp"), None), P(None, ("lang", "dp"), None), P("lang"))
    return jax.shard_map(
        functools.partial(per_device, snake_ring(mesh)), mesh=mesh, in_specs=in_specs, out_specs=out_specs, check_vma=False
    )
```

```python
import functools
import math

import jax
import jax.numpy as jnp
from jax import lax
from jax.sharding import PartitionSpec as P

MARGIN = 0.3
LOW_FILL = -1e30
BLOCK_BYTES = 8 * 1024 * 1024


def target_index(col_count, row_count, per_slot, data_size):
    position = jnp.arange(col_count, dtype=jnp.int32)
    source = position // row_count
    within = position % row_count
    return (within // per_slot * data_size + source) * per_slot + within % per_slot


def snake_ring(mesh):
    count = mesh.shape["dp"]
    try:
        spots = [tuple(dev.coords) for dev in mesh.devices.reshape(-1, count)[0]]
    except (AttributeError, TypeError):
        return list(range(count))
    ys = sorted({s[1] for s in spots})
    zs = sorted({s[2] for s in spots})
    where = {(s[1], s[2]): d for d, s in enumerate(spots)}
    if len(where) != count or len(ys) * len(zs) != count:
        return list(range(count))
    rows, cols = (ys, zs) if len(ys) % 2 == 0 else (zs, ys)
    at = lambda r, c: where[(r, c) if rows is ys else (c, r)]
    if len(rows) == 1 or len(cols) == 1:
        return [at(r, c) for r in rows for c in cols]
    order = [at(rows[0], cols[0])]
    for k, r in enumerate(rows):
        seq = cols[1:] if k % 2 == 0 else cols[:0:-1]
        order += [at(r, c) for c in seq]
    order += [at(r, cols[0]) for r in rows[:0:-1]]
    return order


def ring_gather(block, ring):
    count = len(ring)
    place = [0] * count
    for p, d in enumerate(ring):
        place[d] = p
    ring_arr = jnp.array(ring, jnp.int32)
    my_dp = lax.axis_index("dp")
    my_pos = jnp.array(place, jnp.int32)[my_dp]
    ahead = [(ring[p], ring[(p + 1) % count]) for p in range(count)]
    behind = [(ring[p], ring[(p - 1) % count]) for p in range(count)]
    rows = block.shape[0]
    out = jnp.zeros((count * rows,) + block.shape[1:], block.dtype)
    out = lax.dynamic_update_slice_in_dim(out, block, my_dp * rows, 0)
    for pairs, steps, sign in ((ahead, count // 2, -1), (behind, count - 1 - count // 2, 1)):
        cur = block
        for t in range(1, steps + 1):
            cur = lax.ppermute(cur, "dp", pairs)
            origin = ring_arr[(my_pos + sign * t) % count]
            out = lax.dynamic_update_slice_in_dim(out, cur, origin * rows, 0)
    return out


def scores_of(x_rows, y_rows, pos_mask, inv_root):
    raw_dot = lax.dot_general(
        x_rows, y_rows, (((1,), (1,)), ((), ())), preferred_element_type=jnp.float32
    )
    return raw_dot * inv_root - MARGIN * pos_mask.astype(jnp.float32)


def block_stats(scores_f, is_pos, row_live, col_ok):
    row_max = jnp.max(jnp.where(col_ok[None, :], scores_f, LOW_FILL), axis=1)
    row_sum = jnp.sum(
        jnp.where(col_ok[None, :], jnp.exp(scores_f - row_max[:, None]), 0.0), axis=1
    )
    row_lse = row_max + jnp.log(row_sum + (1.0 - row_live.astype(jnp.float32)))
    pos_score = jnp.sum(jnp.where(is_pos, scores_f, 0.0), axis=1)
    col_max = jnp.max(jnp.where(row_live[:, None], scores_f, LOW_FILL), axis=0)
    col_sum = jnp.sum(
        jnp.where(row_live[:, None], jnp.exp(scores_f - col_max[None, :]), 0.0), axis=0
    )
    return row_lse, pos_score, col_max, col_sum


def grad_of(scores_f, is_pos, row_ok, col_ok, row_lse, col_lse, weight):
    both_live = row_ok[:, None] & col_ok[None, :]
    by_row = jnp.where(both_live, jnp.exp(scores_f - row_lse[:, None]), 0.0)
    by_col = jnp.where(both_live, jnp.exp(scores_f - col_lse[None, :]), 0.0)
    pos_hit = (is_pos & row_ok[:, None]).astype(jnp.float32)
    return (weight * (by_row + by_col - 2.0 * pos_hit)).astype(jnp.bfloat16)


def per_device(ring, src_emb, tgt_emb, slot_group, counts, align, pair_weight):
    lang_size = lax.axis_size("lang")
    data_size = lax.axis_size("dp")
    row_count, emb_width = src_emb.shape
    per_slot = tgt_emb.shape[1]
    pair_rows = row_count * data_size
    inv_root = 1.0 / math.sqrt(emb_width)
    group_index = lax.axis_index("lang")
    shard_index = lax.axis_index("dp")
    slot_ids = jnp.arange(lang_size, dtype=jnp.int32)
    slot_of_group = jnp.zeros((lang_size,), jnp.int32).at[slot_group].set(slot_ids)
    ordered = tgt_emb[slot_of_group]
    arrived = lax.all_to_all(ordered, "lang", split_axis=0, concat_axis=1, tiled=True)
    partner = arrived[0]
    live_count = counts[group_index]
    weight = pair_weight[group_index]
    pair_align = align[0]
    all_rows = jnp.arange(pair_rows, dtype=jnp.int32)
    row_live = all_rows < live_count
    perm = target_index(pair_rows, row_count, per_slot, data_size)
    live_pos = (perm[None, :] == pair_align[:, None]) & row_live[:, None]
    col_live = jnp.max(live_pos.astype(jnp.int32), axis=0) > 0
    both = ring_gather(jnp.concatenate([src_emb, partner], 0), ring)
    both = both.reshape(data_size, 2, row_count, emb_width)
    x_all = both[:, 0].reshape(pair_rows, emb_width)
    y_all = both[:, 1].reshape(pair_rows, emb_width)

    block = max(1, min(pair_rows, BLOCK_BYTES // (4 * pair_rows)))
    steps = pair_rows // block
    if steps == 1:
        is_pos = perm[None, :] == pair_align[:, None]
        scores_f = scores_of(x_all, y_all, is_pos, inv_root)
        row_lse, pos_score, col_max, col_sum = block_stats(scores_f, is_pos, row_live, col_live)
    else:
        def one_block(k, carry):
            row_lse, pos_score, col_max, col_sum = carry
            start = k * block
            x_blk = lax.dynamic_slice_in_dim(x_all, start, block)
            a_blk = lax.dynamic_slice_in_dim(pair_align, start, block)
            r_blk = lax.dynamic_slice_in_dim(row_live, start, block)
            is_pos = perm[None, :] == a_blk[:, None]
            s_blk = scores_of(x_blk, y_all, is_pos, inv_root)
            b_lse, b_pos, b_max, b_sum = block_stats(s_blk, is_pos, r_blk, col_live)
            top = jnp.maximum(col_max, b_max)
            col_sum = col_sum * jnp.exp(col_max - top) + b_sum * jnp.exp(b_max - top)
            row_lse = lax.dynamic_update_slice_in_dim(row_lse, b_lse, start, 0)
            pos_score = lax.dynamic_update_slice_in_dim(pos_score, b_pos, start, 0)
            return row_lse, pos_score, top, col_sum

        zeros = jnp.zeros((pair_rows,), jnp.float32)
        init = (zeros, zeros, jnp.full((pair_rows,), LOW_FILL, jnp.float32), zeros)
        row_lse, pos_score, col_max, col_sum = lax.fori_loop(0, steps, one_block, init)
    col_lse = col_max + jnp.log(col_sum + (1.0 - col_live.astype(jnp.float32)))

    row_f = row_live.astype(jnp.float32)
    col_f = col_live.astype(jnp.float32)
    total = jnp.sum(row_f * (row_lse - 2.0 * pos_score)) + jnp.sum(col_f * col_lse)
    pair_loss = (total / live_count.astype(jnp.float32)).reshape(1)

    mine = shard_index * row_count
    a_my = lax.dynamic_slice_in_dim(pair_align, mine, row_count)
    r_my = lax.dynamic_slice_in_dim(row_live, mine, row_count)
    lse_my = lax.dynamic_slice_in_dim(row_lse, mine, row_count)
    pos_rows = perm[None, :] == a_my[:, None]
    s_rows = scores_of(src_emb, y_all, pos_rows, inv_root)
    g_rows = grad_of(s_rows, pos_rows, r_my, col_live, lse_my, col_lse, weight)
    grad_src = (
        jnp.dot(g_rows, y_all, preferred_element_type=jnp.float32) * inv_root
    ).astype(jnp.bfloat16)

    p_my = lax.dynamic_slice_in_dim(perm, mine, row_count)
    c_my = lax.dynamic_slice_in_dim(col_live, mine, row_count)
    clse_my = lax.dynamic_slice_in_dim(col_lse, mine, row_count)
    pos_cols = p_my[None, :] == pair_align[:, None]
    s_cols = scores_of(x_all, partner, pos_cols, inv_root)
    g_cols = grad_of(s_cols, pos_cols, row_live, c_my, row_lse, clse_my, weight)
    own_terms = lax.dot_general(
        g_cols, x_all, (((0,), (0,)), ((), ())), preferred_element_type=jnp.float32
    )
    grad_local = (own_terms * inv_root).astype(jnp.bfloat16)
    returned = lax.all_to_all(
        grad_local.reshape(lang_size, per_slot, emb_width), "lang", split_axis=0, concat_axis=0, tiled=True
    )
    grad_tgt = returned[slot_group]
    return (grad_src, grad_tgt, pair_loss)


def solution(mesh):
    in_specs = (
        P(("lang", "dp"), None),
        P(None, ("lang", "dp"), None),
        P(),
        P(),
        P("lang", None),
        P(),
    )
    out_specs = (P(("lang", "dp"), None), P(None, ("lang", "dp"), None), P("lang"))
    return jax.shard_map(
        functools.partial(per_device, snake_ring(mesh)), mesh=mesh, in_specs=in_specs, out_specs=out_specs, check_vma=False
    )
```

```python
import functools
import math

import jax
import jax.numpy as jnp
from jax import lax
from jax.sharding import PartitionSpec as P

MARGIN = 0.3
LOW_FILL = -1e30
BLOCK_BYTES = 8 * 1024 * 1024


def target_index(col_count, row_count, per_slot, data_size):
    position = jnp.arange(col_count, dtype=jnp.int32)
    source = position // row_count
    within = position % row_count
    return (within // per_slot * data_size + source) * per_slot + within % per_slot


def snake_ring(mesh):
    count = mesh.shape["dp"]
    try:
        spots = [tuple(dev.coords) for dev in mesh.devices.reshape(-1, count)[0]]
    except (AttributeError, TypeError):
        return list(range(count))
    ys = sorted({s[1] for s in spots})
    zs = sorted({s[2] for s in spots})
    where = {(s[1], s[2]): d for d, s in enumerate(spots)}
    if len(where) != count or len(ys) * len(zs) != count:
        return list(range(count))
    rows, cols = (ys, zs) if len(ys) % 2 == 0 else (zs, ys)
    at = lambda r, c: where[(r, c) if rows is ys else (c, r)]
    if len(rows) == 1 or len(cols) == 1:
        return [at(r, c) for r in rows for c in cols]
    order = [at(rows[0], cols[0])]
    for k, r in enumerate(rows):
        seq = cols[1:] if k % 2 == 0 else cols[:0:-1]
        order += [at(r, c) for c in seq]
    order += [at(r, cols[0]) for r in rows[:0:-1]]
    return order


def ring_gather(block, ring):
    count = len(ring)
    place = [0] * count
    for p, d in enumerate(ring):
        place[d] = p
    ring_arr = jnp.array(ring, jnp.int32)
    my_dp = lax.axis_index("dp")
    my_pos = jnp.array(place, jnp.int32)[my_dp]
    ahead = [(ring[p], ring[(p + 1) % count]) for p in range(count)]
    behind = [(ring[p], ring[(p - 1) % count]) for p in range(count)]
    rows = block.shape[0]
    out = jnp.zeros((count * rows,) + block.shape[1:], block.dtype)
    out = lax.dynamic_update_slice_in_dim(out, block, my_dp * rows, 0)
    for pairs, steps, sign in ((ahead, count // 2, -1), (behind, count - 1 - count // 2, 1)):
        cur = block
        for t in range(1, steps + 1):
            cur = lax.ppermute(cur, "dp", pairs)
            origin = ring_arr[(my_pos + sign * t) % count]
            out = lax.dynamic_update_slice_in_dim(out, cur, origin * rows, 0)
    return out


def scores_of(x_rows, y_rows, pos_mask, inv_root):
    raw_dot = lax.dot_general(
        x_rows, y_rows, (((1,), (1,)), ((), ())), preferred_element_type=jnp.float32
    )
    return raw_dot * inv_root - MARGIN * pos_mask.astype(jnp.float32)


def block_stats(scores_f, is_pos, row_live, col_ok):
    row_max = jnp.max(jnp.where(col_ok[None, :], scores_f, LOW_FILL), axis=1)
    row_sum = jnp.sum(
        jnp.where(col_ok[None, :], jnp.exp(scores_f - row_max[:, None]), 0.0), axis=1
    )
    row_lse = row_max + jnp.log(row_sum + (1.0 - row_live.astype(jnp.float32)))
    pos_score = jnp.sum(jnp.where(is_pos, scores_f, 0.0), axis=1)
    col_max = jnp.max(jnp.where(row_live[:, None], scores_f, LOW_FILL), axis=0)
    col_sum = jnp.sum(
        jnp.where(row_live[:, None], jnp.exp(scores_f - col_max[None, :]), 0.0), axis=0
    )
    return row_lse, pos_score, col_max, col_sum


def grad_of(scores_f, is_pos, row_ok, col_ok, row_lse, col_lse, weight):
    both_live = row_ok[:, None] & col_ok[None, :]
    by_row = jnp.where(both_live, jnp.exp(scores_f - row_lse[:, None]), 0.0)
    by_col = jnp.where(both_live, jnp.exp(scores_f - col_lse[None, :]), 0.0)
    pos_hit = (is_pos & row_ok[:, None]).astype(jnp.float32)
    return (weight * (by_row + by_col - 2.0 * pos_hit)).astype(jnp.bfloat16)


def per_device(ring, src_emb, tgt_emb, slot_group, counts, align, pair_weight):
    lang_size = lax.axis_size("lang")
    data_size = lax.axis_size("dp")
    row_count, emb_width = src_emb.shape
    per_slot = tgt_emb.shape[1]
    pair_rows = row_count * data_size
    inv_root = 1.0 / math.sqrt(emb_width)
    group_index = lax.axis_index("lang")
    shard_index = lax.axis_index("dp")
    slot_ids = jnp.arange(lang_size, dtype=jnp.int32)
    slot_of_group = jnp.zeros((lang_size,), jnp.int32).at[slot_group].set(slot_ids)
    partner = jnp.zeros((lang_size * per_slot, emb_width), tgt_emb.dtype)
    own = lax.dynamic_index_in_dim(tgt_emb, slot_of_group[group_index], 0, keepdims=False)
    partner = lax.dynamic_update_slice_in_dim(partner, own, group_index * per_slot, 0)
    for k in range(1, lang_size):
        dest = (group_index + k) % lang_size
        sent = lax.dynamic_index_in_dim(tgt_emb, slot_of_group[dest], 0, keepdims=False)
        got = lax.ppermute(sent, "lang", [(l, (l + k) % lang_size) for l in range(lang_size)])
        origin = (group_index - k) % lang_size
        partner = lax.dynamic_update_slice_in_dim(partner, got, origin * per_slot, 0)
    live_count = counts[group_index]
    weight = pair_weight[group_index]
    pair_align = align[0]
    all_rows = jnp.arange(pair_rows, dtype=jnp.int32)
    row_live = all_rows < live_count
    perm = target_index(pair_rows, row_count, per_slot, data_size)
    live_pos = (perm[None, :] == pair_align[:, None]) & row_live[:, None]
    col_live = jnp.max(live_pos.astype(jnp.int32), axis=0) > 0
    x_all = ring_gather(src_emb, ring)
    y_all = ring_gather(partner, ring)

    block = max(1, min(pair_rows, BLOCK_BYTES // (4 * pair_rows)))
    steps = pair_rows // block
    if steps == 1:
        is_pos = perm[None, :] == pair_align[:, None]
        scores_f = scores_of(x_all, y_all, is_pos, inv_root)
        row_lse, pos_score, col_max, col_sum = block_stats(scores_f, is_pos, row_live, col_live)
    else:
        def one_block(k, carry):
            row_lse, pos_score, col_max, col_sum = carry
            start = k * block
            x_blk = lax.dynamic_slice_in_dim(x_all, start, block)
            a_blk = lax.dynamic_slice_in_dim(pair_align, start, block)
            r_blk = lax.dynamic_slice_in_dim(row_live, start, block)
            is_pos = perm[None, :] == a_blk[:, None]
            s_blk = scores_of(x_blk, y_all, is_pos, inv_root)
            b_lse, b_pos, b_max, b_sum = block_stats(s_blk, is_pos, r_blk, col_live)
            top = jnp.maximum(col_max, b_max)
            col_sum = col_sum * jnp.exp(col_max - top) + b_sum * jnp.exp(b_max - top)
            row_lse = lax.dynamic_update_slice_in_dim(row_lse, b_lse, start, 0)
            pos_score = lax.dynamic_update_slice_in_dim(pos_score, b_pos, start, 0)
            return row_lse, pos_score, top, col_sum

        zeros = jnp.zeros((pair_rows,), jnp.float32)
        init = (zeros, zeros, jnp.full((pair_rows,), LOW_FILL, jnp.float32), zeros)
        row_lse, pos_score, col_max, col_sum = lax.fori_loop(0, steps, one_block, init)
    col_lse = col_max + jnp.log(col_sum + (1.0 - col_live.astype(jnp.float32)))

    row_f = row_live.astype(jnp.float32)
    col_f = col_live.astype(jnp.float32)
    total = jnp.sum(row_f * (row_lse - 2.0 * pos_score)) + jnp.sum(col_f * col_lse)
    pair_loss = (total / live_count.astype(jnp.float32)).reshape(1)

    mine = shard_index * row_count
    a_my = lax.dynamic_slice_in_dim(pair_align, mine, row_count)
    r_my = lax.dynamic_slice_in_dim(row_live, mine, row_count)
    lse_my = lax.dynamic_slice_in_dim(row_lse, mine, row_count)
    pos_rows = perm[None, :] == a_my[:, None]
    s_rows = scores_of(src_emb, y_all, pos_rows, inv_root)
    g_rows = grad_of(s_rows, pos_rows, r_my, col_live, lse_my, col_lse, weight)
    grad_src = (
        jnp.dot(g_rows, y_all, preferred_element_type=jnp.float32) * inv_root
    ).astype(jnp.bfloat16)

    p_my = lax.dynamic_slice_in_dim(perm, mine, row_count)
    c_my = lax.dynamic_slice_in_dim(col_live, mine, row_count)
    clse_my = lax.dynamic_slice_in_dim(col_lse, mine, row_count)
    pos_cols = p_my[None, :] == pair_align[:, None]
    s_cols = scores_of(x_all, partner, pos_cols, inv_root)
    g_cols = grad_of(s_cols, pos_cols, row_live, c_my, row_lse, clse_my, weight)
    own_terms = lax.dot_general(
        g_cols, x_all, (((0,), (0,)), ((), ())), preferred_element_type=jnp.float32
    )
    grad_local = (own_terms * inv_root).astype(jnp.bfloat16)
    returned = lax.all_to_all(
        grad_local.reshape(lang_size, per_slot, emb_width), "lang", split_axis=0, concat_axis=0, tiled=True
    )
    grad_tgt = returned[slot_group]
    return (grad_src, grad_tgt, pair_loss)


def solution(mesh):
    in_specs = (
        P(("lang", "dp"), None),
        P(None, ("lang", "dp"), None),
        P(),
        P(),
        P("lang", None),
        P(),
    )
    out_specs = (P(("lang", "dp"), None), P(None, ("lang", "dp"), None), P("lang"))
    return jax.shard_map(
        functools.partial(per_device, snake_ring(mesh)), mesh=mesh, in_specs=in_specs, out_specs=out_specs, check_vma=False
    )
```

```python
import functools
import math

import jax
import jax.numpy as jnp
from jax import lax
from jax.sharding import PartitionSpec as P

MARGIN = 0.3
LOW_FILL = -1e30
BLOCK_BYTES = 8 * 1024 * 1024


def target_index(col_count, row_count, per_slot, data_size):
    position = jnp.arange(col_count, dtype=jnp.int32)
    source = position // row_count
    within = position % row_count
    return (within // per_slot * data_size + source) * per_slot + within % per_slot


def snake_ring(mesh):
    count = mesh.shape["dp"]
    try:
        spots = [tuple(dev.coords) for dev in mesh.devices.reshape(-1, count)[0]]
    except (AttributeError, TypeError):
        return list(range(count))
    ys = sorted({s[1] for s in spots})
    zs = sorted({s[2] for s in spots})
    where = {(s[1], s[2]): d for d, s in enumerate(spots)}
    if len(where) != count or len(ys) * len(zs) != count:
        return list(range(count))
    rows, cols = (ys, zs) if len(ys) % 2 == 0 else (zs, ys)
    at = lambda r, c: where[(r, c) if rows is ys else (c, r)]
    if len(rows) == 1 or len(cols) == 1:
        return [at(r, c) for r in rows for c in cols]
    order = [at(rows[0], cols[0])]
    for k, r in enumerate(rows):
        seq = cols[1:] if k % 2 == 0 else cols[:0:-1]
        order += [at(r, c) for c in seq]
    order += [at(r, cols[0]) for r in rows[:0:-1]]
    return order


def pick(table, index):
    found = jnp.int32(table[0])
    for k in range(1, len(table)):
        found = jnp.where(index == k, jnp.int32(table[k]), found)
    return found


def slot_rows(tgt_emb, slot_group, group):
    rows = tgt_emb[0]
    for s in range(1, tgt_emb.shape[0]):
        rows = jnp.where(slot_group[s] == group, tgt_emb[s], rows)
    return rows


def ring_gather(block, ring):
    count = len(ring)
    place = [0] * count
    for p, d in enumerate(ring):
        place[d] = p
    my_dp = lax.axis_index("dp")
    my_pos = pick(place, my_dp)
    ahead = [(ring[p], ring[(p + 1) % count]) for p in range(count)]
    behind = [(ring[p], ring[(p - 1) % count]) for p in range(count)]
    rows = block.shape[0]
    out = jnp.zeros((count * rows,) + block.shape[1:], block.dtype)
    out = lax.dynamic_update_slice_in_dim(out, block, my_dp * rows, 0)
    for pairs, steps, sign in ((ahead, count // 2, -1), (behind, count - 1 - count // 2, 1)):
        cur = block
        for t in range(1, steps + 1):
            cur = lax.ppermute(cur, "dp", pairs)
            origin = pick(ring, (my_pos + sign * t) % count)
            out = lax.dynamic_update_slice_in_dim(out, cur, origin * rows, 0)
    return out


def scores_of(x_rows, y_rows, pos_mask, inv_root):
    raw_dot = lax.dot_general(
        x_rows, y_rows, (((1,), (1,)), ((), ())), preferred_element_type=jnp.float32
    )
    return raw_dot * inv_root - MARGIN * pos_mask.astype(jnp.float32)


def block_stats(scores_f, is_pos, row_live, col_ok):
    row_max = jnp.max(jnp.where(col_ok[None, :], scores_f, LOW_FILL), axis=1)
    row_sum = jnp.sum(
        jnp.where(col_ok[None, :], jnp.exp(scores_f - row_max[:, None]), 0.0), axis=1
    )
    row_lse = row_max + jnp.log(row_sum + (1.0 - row_live.astype(jnp.float32)))
    pos_score = jnp.sum(jnp.where(is_pos, scores_f, 0.0), axis=1)
    col_max = jnp.max(jnp.where(row_live[:, None], scores_f, LOW_FILL), axis=0)
    col_sum = jnp.sum(
        jnp.where(row_live[:, None], jnp.exp(scores_f - col_max[None, :]), 0.0), axis=0
    )
    return row_lse, pos_score, col_max, col_sum


def grad_of(scores_f, is_pos, row_ok, col_ok, row_lse, col_lse, weight):
    both_live = row_ok[:, None] & col_ok[None, :]
    by_row = jnp.where(both_live, jnp.exp(scores_f - row_lse[:, None]), 0.0)
    by_col = jnp.where(both_live, jnp.exp(scores_f - col_lse[None, :]), 0.0)
    pos_hit = (is_pos & row_ok[:, None]).astype(jnp.float32)
    return (weight * (by_row + by_col - 2.0 * pos_hit)).astype(jnp.bfloat16)


def per_device(ring, src_emb, tgt_emb, slot_group, counts, align, pair_weight):
    lang_size = lax.axis_size("lang")
    data_size = lax.axis_size("dp")
    row_count, emb_width = src_emb.shape
    per_slot = tgt_emb.shape[1]
    pair_rows = row_count * data_size
    inv_root = 1.0 / math.sqrt(emb_width)
    group_index = lax.axis_index("lang")
    shard_index = lax.axis_index("dp")
    partner = jnp.zeros((lang_size * per_slot, emb_width), tgt_emb.dtype)
    own = slot_rows(tgt_emb, slot_group, group_index)
    partner = lax.dynamic_update_slice_in_dim(partner, own, group_index * per_slot, 0)
    for k in range(1, lang_size):
        dest = (group_index + k) % lang_size
        sent = slot_rows(tgt_emb, slot_group, dest)
        got = lax.ppermute(sent, "lang", [(l, (l + k) % lang_size) for l in range(lang_size)])
        origin = (group_index - k) % lang_size
        partner = lax.dynamic_update_slice_in_dim(partner, got, origin * per_slot, 0)
    live_count = counts[group_index]
    weight = pair_weight[group_index]
    pair_align = align[0]
    all_rows = jnp.arange(pair_rows, dtype=jnp.int32)
    row_live = all_rows < live_count
    perm = target_index(pair_rows, row_count, per_slot, data_size)
    live_pos = (perm[None, :] == pair_align[:, None]) & row_live[:, None]
    col_live = jnp.max(live_pos.astype(jnp.int32), axis=0) > 0
    x_all = ring_gather(src_emb, ring)
    y_all = ring_gather(partner, ring)

    block = max(1, min(pair_rows, BLOCK_BYTES // (4 * pair_rows)))
    steps = pair_rows // block
    if steps == 1:
        is_pos = perm[None, :] == pair_align[:, None]
        scores_f = scores_of(x_all, y_all, is_pos, inv_root)
        row_lse, pos_score, col_max, col_sum = block_stats(scores_f, is_pos, row_live, col_live)
    else:
        def one_block(k, carry):
            row_lse, pos_score, col_max, col_sum = carry
            start = k * block
            x_blk = lax.dynamic_slice_in_dim(x_all, start, block)
            a_blk = lax.dynamic_slice_in_dim(pair_align, start, block)
            r_blk = lax.dynamic_slice_in_dim(row_live, start, block)
            is_pos = perm[None, :] == a_blk[:, None]
            s_blk = scores_of(x_blk, y_all, is_pos, inv_root)
            b_lse, b_pos, b_max, b_sum = block_stats(s_blk, is_pos, r_blk, col_live)
            top = jnp.maximum(col_max, b_max)
            col_sum = col_sum * jnp.exp(col_max - top) + b_sum * jnp.exp(b_max - top)
            row_lse = lax.dynamic_update_slice_in_dim(row_lse, b_lse, start, 0)
            pos_score = lax.dynamic_update_slice_in_dim(pos_score, b_pos, start, 0)
            return row_lse, pos_score, top, col_sum

        zeros = jnp.zeros((pair_rows,), jnp.float32)
        init = (zeros, zeros, jnp.full((pair_rows,), LOW_FILL, jnp.float32), zeros)
        row_lse, pos_score, col_max, col_sum = lax.fori_loop(0, steps, one_block, init)
    col_lse = col_max + jnp.log(col_sum + (1.0 - col_live.astype(jnp.float32)))

    row_f = row_live.astype(jnp.float32)
    col_f = col_live.astype(jnp.float32)
    total = jnp.sum(row_f * (row_lse - 2.0 * pos_score)) + jnp.sum(col_f * col_lse)
    pair_loss = (total / live_count.astype(jnp.float32)).reshape(1)

    mine = shard_index * row_count
    a_my = lax.dynamic_slice_in_dim(pair_align, mine, row_count)
    r_my = lax.dynamic_slice_in_dim(row_live, mine, row_count)
    lse_my = lax.dynamic_slice_in_dim(row_lse, mine, row_count)
    pos_rows = perm[None, :] == a_my[:, None]
    s_rows = scores_of(src_emb, y_all, pos_rows, inv_root)
    g_rows = grad_of(s_rows, pos_rows, r_my, col_live, lse_my, col_lse, weight)
    grad_src = (
        jnp.dot(g_rows, y_all, preferred_element_type=jnp.float32) * inv_root
    ).astype(jnp.bfloat16)

    p_my = lax.dynamic_slice_in_dim(perm, mine, row_count)
    c_my = lax.dynamic_slice_in_dim(col_live, mine, row_count)
    clse_my = lax.dynamic_slice_in_dim(col_lse, mine, row_count)
    pos_cols = p_my[None, :] == pair_align[:, None]
    s_cols = scores_of(x_all, partner, pos_cols, inv_root)
    g_cols = grad_of(s_cols, pos_cols, row_live, c_my, row_lse, clse_my, weight)
    own_terms = lax.dot_general(
        g_cols, x_all, (((0,), (0,)), ((), ())), preferred_element_type=jnp.float32
    )
    grad_local = (own_terms * inv_root).astype(jnp.bfloat16)
    returned = lax.all_to_all(
        grad_local.reshape(lang_size, per_slot, emb_width), "lang", split_axis=0, concat_axis=0, tiled=True
    )
    grad_tgt = jnp.stack(
        [slot_rows(returned, jnp.arange(lang_size, dtype=jnp.int32), slot_group[s]) for s in range(lang_size)]
    )
    return (grad_src, grad_tgt, pair_loss)


def solution(mesh):
    in_specs = (
        P(("lang", "dp"), None),
        P(None, ("lang", "dp"), None),
        P(),
        P(),
        P("lang", None),
        P(),
    )
    out_specs = (P(("lang", "dp"), None), P(None, ("lang", "dp"), None), P("lang"))
    return jax.shard_map(
        functools.partial(per_device, snake_ring(mesh)), mesh=mesh, in_specs=in_specs, out_specs=out_specs, check_vma=False
    )
```

```python
import functools
import math

import jax
import jax.numpy as jnp
from jax import lax
from jax.sharding import PartitionSpec as P

MARGIN = 0.3
LOW_FILL = -1e30
BLOCK_BYTES = 8 * 1024 * 1024


def target_index(col_count, row_count, per_slot, data_size):
    position = jnp.arange(col_count, dtype=jnp.int32)
    source = position // row_count
    within = position % row_count
    return (within // per_slot * data_size + source) * per_slot + within % per_slot


def snake_ring(mesh):
    count = mesh.shape["dp"]
    try:
        spots = [tuple(dev.coords) for dev in mesh.devices.reshape(-1, count)[0]]
    except (AttributeError, TypeError):
        return list(range(count))
    ys = sorted({s[1] for s in spots})
    zs = sorted({s[2] for s in spots})
    where = {(s[1], s[2]): d for d, s in enumerate(spots)}
    if len(where) != count or len(ys) * len(zs) != count:
        return list(range(count))
    rows, cols = (ys, zs) if len(ys) % 2 == 0 else (zs, ys)
    at = lambda r, c: where[(r, c) if rows is ys else (c, r)]
    if len(rows) == 1 or len(cols) == 1:
        return [at(r, c) for r in rows for c in cols]
    order = [at(rows[0], cols[0])]
    for k, r in enumerate(rows):
        seq = cols[1:] if k % 2 == 0 else cols[:0:-1]
        order += [at(r, c) for c in seq]
    order += [at(r, cols[0]) for r in rows[:0:-1]]
    return order


def pick(table, index):
    found = jnp.int32(table[0])
    for k in range(1, len(table)):
        found = jnp.where(index == k, jnp.int32(table[k]), found)
    return found


def slot_rows(tgt_emb, slot_group, group):
    rows = tgt_emb[0]
    for s in range(1, tgt_emb.shape[0]):
        rows = jnp.where(slot_group[s] == group, tgt_emb[s], rows)
    return rows


def ring_gather(block, ring):
    count = len(ring)
    place = [0] * count
    for p, d in enumerate(ring):
        place[d] = p
    my_dp = lax.axis_index("dp")
    my_pos = pick(place, my_dp)
    ahead = [(ring[p], ring[(p + 1) % count]) for p in range(count)]
    behind = [(ring[p], ring[(p - 1) % count]) for p in range(count)]
    rows = block.shape[0]
    out = jnp.zeros((count * rows,) + block.shape[1:], block.dtype)
    out = lax.dynamic_update_slice_in_dim(out, block, my_dp * rows, 0)
    for pairs, steps, sign in ((ahead, count // 2, -1), (behind, count - 1 - count // 2, 1)):
        cur = block
        for t in range(1, steps + 1):
            cur = lax.ppermute(cur, "dp", pairs)
            origin = pick(ring, (my_pos + sign * t) % count)
            out = lax.dynamic_update_slice_in_dim(out, cur, origin * rows, 0)
    return out


def scores_of(x_rows, y_rows, pos_mask, inv_root):
    raw_dot = lax.dot_general(
        x_rows, y_rows, (((1,), (1,)), ((), ())), preferred_element_type=jnp.float32
    )
    return raw_dot * inv_root - MARGIN * pos_mask.astype(jnp.float32)


def block_stats(scores_f, is_pos, row_live, col_ok):
    row_max = jnp.max(jnp.where(col_ok[None, :], scores_f, LOW_FILL), axis=1)
    row_sum = jnp.sum(
        jnp.where(col_ok[None, :], jnp.exp(scores_f - row_max[:, None]), 0.0), axis=1
    )
    row_lse = row_max + jnp.log(row_sum + (1.0 - row_live.astype(jnp.float32)))
    pos_score = jnp.sum(jnp.where(is_pos, scores_f, 0.0), axis=1)
    col_max = jnp.max(jnp.where(row_live[:, None], scores_f, LOW_FILL), axis=0)
    col_sum = jnp.sum(
        jnp.where(row_live[:, None], jnp.exp(scores_f - col_max[None, :]), 0.0), axis=0
    )
    return row_lse, pos_score, col_max, col_sum


def grad_of(scores_f, is_pos, row_ok, col_ok, row_lse, col_lse, weight):
    both_live = row_ok[:, None] & col_ok[None, :]
    by_row = jnp.where(both_live, jnp.exp(scores_f - row_lse[:, None]), 0.0)
    by_col = jnp.where(both_live, jnp.exp(scores_f - col_lse[None, :]), 0.0)
    pos_hit = (is_pos & row_ok[:, None]).astype(jnp.float32)
    return (weight * (by_row + by_col - 2.0 * pos_hit)).astype(jnp.bfloat16)


def per_device(ring, src_emb, tgt_emb, slot_group, counts, align, pair_weight):
    lang_size = lax.axis_size("lang")
    data_size = lax.axis_size("dp")
    row_count, emb_width = src_emb.shape
    per_slot = tgt_emb.shape[1]
    pair_rows = row_count * data_size
    inv_root = 1.0 / math.sqrt(emb_width)
    group_index = lax.axis_index("lang")
    shard_index = lax.axis_index("dp")
    partner = jnp.zeros((lang_size * per_slot, emb_width), tgt_emb.dtype)
    own = slot_rows(tgt_emb, slot_group, group_index)
    partner = lax.dynamic_update_slice_in_dim(partner, own, group_index * per_slot, 0)
    for k in range(1, lang_size):
        dest = (group_index + k) % lang_size
        sent = slot_rows(tgt_emb, slot_group, dest)
        got = lax.ppermute(sent, "lang", [(l, (l + k) % lang_size) for l in range(lang_size)])
        origin = (group_index - k) % lang_size
        partner = lax.dynamic_update_slice_in_dim(partner, got, origin * per_slot, 0)
    live_count = counts[group_index]
    weight = pair_weight[group_index]
    pair_align = align[0]
    all_rows = jnp.arange(pair_rows, dtype=jnp.int32)
    row_live = all_rows < live_count
    perm = target_index(pair_rows, row_count, per_slot, data_size)
    live_pos = (perm[None, :] == pair_align[:, None]) & row_live[:, None]
    col_live = jnp.max(live_pos.astype(jnp.int32), axis=0) > 0
    after = src_emb + jnp.zeros_like(src_emb) * partner[:1, :1]
    x_all = ring_gather(after, ring)
    y_all = ring_gather(partner, ring)

    block = max(1, min(pair_rows, BLOCK_BYTES // (4 * pair_rows)))
    steps = pair_rows // block
    if steps == 1:
        is_pos = perm[None, :] == pair_align[:, None]
        scores_f = scores_of(x_all, y_all, is_pos, inv_root)
        row_lse, pos_score, col_max, col_sum = block_stats(scores_f, is_pos, row_live, col_live)
    else:
        def one_block(k, carry):
            row_lse, pos_score, col_max, col_sum = carry
            start = k * block
            x_blk = lax.dynamic_slice_in_dim(x_all, start, block)
            a_blk = lax.dynamic_slice_in_dim(pair_align, start, block)
            r_blk = lax.dynamic_slice_in_dim(row_live, start, block)
            is_pos = perm[None, :] == a_blk[:, None]
            s_blk = scores_of(x_blk, y_all, is_pos, inv_root)
            b_lse, b_pos, b_max, b_sum = block_stats(s_blk, is_pos, r_blk, col_live)
            top = jnp.maximum(col_max, b_max)
            col_sum = col_sum * jnp.exp(col_max - top) + b_sum * jnp.exp(b_max - top)
            row_lse = lax.dynamic_update_slice_in_dim(row_lse, b_lse, start, 0)
            pos_score = lax.dynamic_update_slice_in_dim(pos_score, b_pos, start, 0)
            return row_lse, pos_score, top, col_sum

        zeros = jnp.zeros((pair_rows,), jnp.float32)
        init = (zeros, zeros, jnp.full((pair_rows,), LOW_FILL, jnp.float32), zeros)
        row_lse, pos_score, col_max, col_sum = lax.fori_loop(0, steps, one_block, init)
    col_lse = col_max + jnp.log(col_sum + (1.0 - col_live.astype(jnp.float32)))

    row_f = row_live.astype(jnp.float32)
    col_f = col_live.astype(jnp.float32)
    total = jnp.sum(row_f * (row_lse - 2.0 * pos_score)) + jnp.sum(col_f * col_lse)
    pair_loss = (total / live_count.astype(jnp.float32)).reshape(1)

    mine = shard_index * row_count
    a_my = lax.dynamic_slice_in_dim(pair_align, mine, row_count)
    r_my = lax.dynamic_slice_in_dim(row_live, mine, row_count)
    lse_my = lax.dynamic_slice_in_dim(row_lse, mine, row_count)
    pos_rows = perm[None, :] == a_my[:, None]
    s_rows = scores_of(src_emb, y_all, pos_rows, inv_root)
    g_rows = grad_of(s_rows, pos_rows, r_my, col_live, lse_my, col_lse, weight)
    grad_src = (
        jnp.dot(g_rows, y_all, preferred_element_type=jnp.float32) * inv_root
    ).astype(jnp.bfloat16)

    p_my = lax.dynamic_slice_in_dim(perm, mine, row_count)
    c_my = lax.dynamic_slice_in_dim(col_live, mine, row_count)
    clse_my = lax.dynamic_slice_in_dim(col_lse, mine, row_count)
    pos_cols = p_my[None, :] == pair_align[:, None]
    s_cols = scores_of(x_all, partner, pos_cols, inv_root)
    g_cols = grad_of(s_cols, pos_cols, row_live, c_my, row_lse, clse_my, weight)
    own_terms = lax.dot_general(
        g_cols, x_all, (((0,), (0,)), ((), ())), preferred_element_type=jnp.float32
    )
    grad_local = (own_terms * inv_root).astype(jnp.bfloat16)
    returned = lax.all_to_all(
        grad_local.reshape(lang_size, per_slot, emb_width), "lang", split_axis=0, concat_axis=0, tiled=True
    )
    grad_tgt = jnp.stack(
        [slot_rows(returned, jnp.arange(lang_size, dtype=jnp.int32), slot_group[s]) for s in range(lang_size)]
    )
    return (grad_src, grad_tgt, pair_loss)


def solution(mesh):
    in_specs = (
        P(("lang", "dp"), None),
        P(None, ("lang", "dp"), None),
        P(),
        P(),
        P("lang", None),
        P(),
    )
    out_specs = (P(("lang", "dp"), None), P(None, ("lang", "dp"), None), P("lang"))
    return jax.shard_map(
        functools.partial(per_device, snake_ring(mesh)), mesh=mesh, in_specs=in_specs, out_specs=out_specs, check_vma=False
    )
```

```python
import functools
import math

import jax
import jax.numpy as jnp
from jax import lax
from jax.sharding import PartitionSpec as P

MARGIN = 0.3
LOW_FILL = -1e30
BLOCK_BYTES = 8 * 1024 * 1024


def target_index(col_count, row_count, per_slot, data_size):
    position = jnp.arange(col_count, dtype=jnp.int32)
    source = position // row_count
    within = position % row_count
    return (within // per_slot * data_size + source) * per_slot + within % per_slot


def snake_ring(mesh):
    count = mesh.shape["dp"]
    try:
        spots = [tuple(dev.coords) for dev in mesh.devices.reshape(-1, count)[0]]
    except (AttributeError, TypeError):
        return list(range(count))
    ys = sorted({s[1] for s in spots})
    zs = sorted({s[2] for s in spots})
    where = {(s[1], s[2]): d for d, s in enumerate(spots)}
    if len(where) != count or len(ys) * len(zs) != count:
        return list(range(count))
    rows, cols = (ys, zs) if len(ys) % 2 == 0 else (zs, ys)
    at = lambda r, c: where[(r, c) if rows is ys else (c, r)]
    if len(rows) == 1 or len(cols) == 1:
        return [at(r, c) for r in rows for c in cols]
    order = [at(rows[0], cols[0])]
    for k, r in enumerate(rows):
        seq = cols[1:] if k % 2 == 0 else cols[:0:-1]
        order += [at(r, c) for c in seq]
    order += [at(r, cols[0]) for r in rows[:0:-1]]
    return order


def pick(table, index):
    found = jnp.int32(table[0])
    for k in range(1, len(table)):
        found = jnp.where(index == k, jnp.int32(table[k]), found)
    return found


def slot_rows(tgt_emb, slot_group, group):
    rows = tgt_emb[0]
    for s in range(1, tgt_emb.shape[0]):
        rows = jnp.where(slot_group[s] == group, tgt_emb[s], rows)
    return rows


def ring_gather(block, ring):
    count = len(ring)
    place = [0] * count
    for p, d in enumerate(ring):
        place[d] = p
    my_dp = lax.axis_index("dp")
    my_pos = pick(place, my_dp)
    ahead = [(ring[p], ring[(p + 1) % count]) for p in range(count)]
    behind = [(ring[p], ring[(p - 1) % count]) for p in range(count)]
    rows = block.shape[0]
    out = jnp.zeros((count * rows,) + block.shape[1:], block.dtype)
    out = lax.dynamic_update_slice_in_dim(out, block, my_dp * rows, 0)
    for pairs, steps, sign in ((ahead, count // 2, -1), (behind, count - 1 - count // 2, 1)):
        cur = block
        for t in range(1, steps + 1):
            cur = lax.ppermute(cur, "dp", pairs)
            origin = pick(ring, (my_pos + sign * t) % count)
            out = lax.dynamic_update_slice_in_dim(out, cur, origin * rows, 0)
    return out


def scores_of(x_rows, y_rows, pos_mask, inv_root):
    raw_dot = lax.dot_general(
        x_rows, y_rows, (((1,), (1,)), ((), ())), preferred_element_type=jnp.float32
    )
    return raw_dot * inv_root - MARGIN * pos_mask.astype(jnp.float32)


def block_stats(scores_f, is_pos, row_live, col_ok):
    row_max = jnp.max(jnp.where(col_ok[None, :], scores_f, LOW_FILL), axis=1)
    row_sum = jnp.sum(
        jnp.where(col_ok[None, :], jnp.exp(scores_f - row_max[:, None]), 0.0), axis=1
    )
    row_lse = row_max + jnp.log(row_sum + (1.0 - row_live.astype(jnp.float32)))
    pos_score = jnp.sum(jnp.where(is_pos, scores_f, 0.0), axis=1)
    col_max = jnp.max(jnp.where(row_live[:, None], scores_f, LOW_FILL), axis=0)
    col_sum = jnp.sum(
        jnp.where(row_live[:, None], jnp.exp(scores_f - col_max[None, :]), 0.0), axis=0
    )
    return row_lse, pos_score, col_max, col_sum


def grad_of(scores_f, is_pos, row_ok, col_ok, row_lse, col_lse, weight):
    both_live = row_ok[:, None] & col_ok[None, :]
    by_row = jnp.where(both_live, jnp.exp(scores_f - row_lse[:, None]), 0.0)
    by_col = jnp.where(both_live, jnp.exp(scores_f - col_lse[None, :]), 0.0)
    pos_hit = (is_pos & row_ok[:, None]).astype(jnp.float32)
    return (weight * (by_row + by_col - 2.0 * pos_hit)).astype(jnp.bfloat16)


def per_device(ring, src_emb, tgt_emb, slot_group, counts, align, pair_weight):
    lang_size = lax.axis_size("lang")
    data_size = lax.axis_size("dp")
    row_count, emb_width = src_emb.shape
    per_slot = tgt_emb.shape[1]
    pair_rows = row_count * data_size
    inv_root = 1.0 / math.sqrt(emb_width)
    group_index = lax.axis_index("lang")
    shard_index = lax.axis_index("dp")
    ordered = jnp.stack([slot_rows(tgt_emb, slot_group, g) for g in range(lang_size)])
    arrived = lax.all_to_all(ordered, "lang", split_axis=0, concat_axis=1, tiled=True)
    partner = arrived[0]
    live_count = counts[group_index]
    weight = pair_weight[group_index]
    pair_align = align[0]
    all_rows = jnp.arange(pair_rows, dtype=jnp.int32)
    row_live = all_rows < live_count
    perm = target_index(pair_rows, row_count, per_slot, data_size)
    live_pos = (perm[None, :] == pair_align[:, None]) & row_live[:, None]
    col_live = jnp.max(live_pos.astype(jnp.int32), axis=0) > 0
    x_all = ring_gather(src_emb, ring)
    y_all = ring_gather(partner, ring)

    block = max(1, min(pair_rows, BLOCK_BYTES // (4 * pair_rows)))
    steps = pair_rows // block
    if steps == 1:
        is_pos = perm[None, :] == pair_align[:, None]
        scores_f = scores_of(x_all, y_all, is_pos, inv_root)
        row_lse, pos_score, col_max, col_sum = block_stats(scores_f, is_pos, row_live, col_live)
    else:
        def one_block(k, carry):
            row_lse, pos_score, col_max, col_sum = carry
            start = k * block
            x_blk = lax.dynamic_slice_in_dim(x_all, start, block)
            a_blk = lax.dynamic_slice_in_dim(pair_align, start, block)
            r_blk = lax.dynamic_slice_in_dim(row_live, start, block)
            is_pos = perm[None, :] == a_blk[:, None]
            s_blk = scores_of(x_blk, y_all, is_pos, inv_root)
            b_lse, b_pos, b_max, b_sum = block_stats(s_blk, is_pos, r_blk, col_live)
            top = jnp.maximum(col_max, b_max)
            col_sum = col_sum * jnp.exp(col_max - top) + b_sum * jnp.exp(b_max - top)
            row_lse = lax.dynamic_update_slice_in_dim(row_lse, b_lse, start, 0)
            pos_score = lax.dynamic_update_slice_in_dim(pos_score, b_pos, start, 0)
            return row_lse, pos_score, top, col_sum

        zeros = jnp.zeros((pair_rows,), jnp.float32)
        init = (zeros, zeros, jnp.full((pair_rows,), LOW_FILL, jnp.float32), zeros)
        row_lse, pos_score, col_max, col_sum = lax.fori_loop(0, steps, one_block, init)
    col_lse = col_max + jnp.log(col_sum + (1.0 - col_live.astype(jnp.float32)))

    row_f = row_live.astype(jnp.float32)
    col_f = col_live.astype(jnp.float32)
    total = jnp.sum(row_f * (row_lse - 2.0 * pos_score)) + jnp.sum(col_f * col_lse)
    pair_loss = (total / live_count.astype(jnp.float32)).reshape(1)

    mine = shard_index * row_count
    a_my = lax.dynamic_slice_in_dim(pair_align, mine, row_count)
    r_my = lax.dynamic_slice_in_dim(row_live, mine, row_count)
    lse_my = lax.dynamic_slice_in_dim(row_lse, mine, row_count)
    pos_rows = perm[None, :] == a_my[:, None]
    s_rows = scores_of(src_emb, y_all, pos_rows, inv_root)
    g_rows = grad_of(s_rows, pos_rows, r_my, col_live, lse_my, col_lse, weight)
    grad_src = (
        jnp.dot(g_rows, y_all, preferred_element_type=jnp.float32) * inv_root
    ).astype(jnp.bfloat16)

    p_my = lax.dynamic_slice_in_dim(perm, mine, row_count)
    c_my = lax.dynamic_slice_in_dim(col_live, mine, row_count)
    clse_my = lax.dynamic_slice_in_dim(col_lse, mine, row_count)
    pos_cols = p_my[None, :] == pair_align[:, None]
    s_cols = scores_of(x_all, partner, pos_cols, inv_root)
    g_cols = grad_of(s_cols, pos_cols, row_live, c_my, row_lse, clse_my, weight)
    own_terms = lax.dot_general(
        g_cols, x_all, (((0,), (0,)), ((), ())), preferred_element_type=jnp.float32
    )
    grad_local = (own_terms * inv_root).astype(jnp.bfloat16)
    returned = lax.all_to_all(
        grad_local.reshape(lang_size, per_slot, emb_width), "lang", split_axis=0, concat_axis=0, tiled=True
    )
    grad_tgt = jnp.stack(
        [slot_rows(returned, jnp.arange(lang_size, dtype=jnp.int32), slot_group[s]) for s in range(lang_size)]
    )
    return (grad_src, grad_tgt, pair_loss)


def solution(mesh):
    in_specs = (
        P(("lang", "dp"), None),
        P(None, ("lang", "dp"), None),
        P(),
        P(),
        P("lang", None),
        P(),
    )
    out_specs = (P(("lang", "dp"), None), P(None, ("lang", "dp"), None), P("lang"))
    return jax.shard_map(
        functools.partial(per_device, snake_ring(mesh)), mesh=mesh, in_specs=in_specs, out_specs=out_specs, check_vma=False
    )
```

```python
import functools
import math

import jax
import jax.numpy as jnp
from jax import lax
from jax.sharding import PartitionSpec as P

MARGIN = 0.3
LOW_FILL = -1e30
BLOCK_BYTES = 8 * 1024 * 1024


def target_index(col_count, row_count, per_slot, data_size):
    position = jnp.arange(col_count, dtype=jnp.int32)
    source = position // row_count
    within = position % row_count
    return (within // per_slot * data_size + source) * per_slot + within % per_slot


def snake_ring(mesh):
    count = mesh.shape["dp"]
    try:
        spots = [tuple(dev.coords) for dev in mesh.devices.reshape(-1, count)[0]]
    except (AttributeError, TypeError):
        return list(range(count))
    ys = sorted({s[1] for s in spots})
    zs = sorted({s[2] for s in spots})
    where = {(s[1], s[2]): d for d, s in enumerate(spots)}
    if len(where) != count or len(ys) * len(zs) != count:
        return list(range(count))
    rows, cols = (ys, zs) if len(ys) % 2 == 0 else (zs, ys)
    at = lambda r, c: where[(r, c) if rows is ys else (c, r)]
    if len(rows) == 1 or len(cols) == 1:
        return [at(r, c) for r in rows for c in cols]
    order = [at(rows[0], cols[0])]
    for k, r in enumerate(rows):
        seq = cols[1:] if k % 2 == 0 else cols[:0:-1]
        order += [at(r, c) for c in seq]
    order += [at(r, cols[0]) for r in rows[:0:-1]]
    return order


def ring_gather(block, ring):
    count = len(ring)
    place = [0] * count
    for p, d in enumerate(ring):
        place[d] = p
    ring_arr = jnp.array(ring, jnp.int32)
    my_dp = lax.axis_index("dp")
    my_pos = jnp.array(place, jnp.int32)[my_dp]
    ahead = [(ring[p], ring[(p + 1) % count]) for p in range(count)]
    behind = [(ring[p], ring[(p - 1) % count]) for p in range(count)]
    rows = block.shape[0]
    out = jnp.zeros((count * rows,) + block.shape[1:], block.dtype)
    out = lax.dynamic_update_slice_in_dim(out, block, my_dp * rows, 0)
    for pairs, steps, sign in ((ahead, count // 2, -1), (behind, count - 1 - count // 2, 1)):
        cur = block
        for t in range(1, steps + 1):
            cur = lax.ppermute(cur, "dp", pairs)
            origin = ring_arr[(my_pos + sign * t) % count]
            out = lax.dynamic_update_slice_in_dim(out, cur, origin * rows, 0)
    return out


def scores_of(x_rows, y_rows, pos_mask, inv_root):
    raw_dot = lax.dot_general(
        x_rows, y_rows, (((1,), (1,)), ((), ())), preferred_element_type=jnp.float32
    )
    return raw_dot * inv_root - MARGIN * pos_mask.astype(jnp.float32)


def block_stats(scores_f, is_pos, row_live, col_ok):
    row_max = jnp.max(jnp.where(col_ok[None, :], scores_f, LOW_FILL), axis=1)
    row_sum = jnp.sum(
        jnp.where(col_ok[None, :], jnp.exp(scores_f - row_max[:, None]), 0.0), axis=1
    )
    row_lse = row_max + jnp.log(row_sum + (1.0 - row_live.astype(jnp.float32)))
    pos_score = jnp.sum(jnp.where(is_pos, scores_f, 0.0), axis=1)
    col_max = jnp.max(jnp.where(row_live[:, None], scores_f, LOW_FILL), axis=0)
    col_sum = jnp.sum(
        jnp.where(row_live[:, None], jnp.exp(scores_f - col_max[None, :]), 0.0), axis=0
    )
    return row_lse, pos_score, col_max, col_sum


def grad_of(scores_f, is_pos, row_ok, col_ok, row_lse, col_lse, weight):
    both_live = row_ok[:, None] & col_ok[None, :]
    by_row = jnp.where(both_live, jnp.exp(scores_f - row_lse[:, None]), 0.0)
    by_col = jnp.where(both_live, jnp.exp(scores_f - col_lse[None, :]), 0.0)
    pos_hit = (is_pos & row_ok[:, None]).astype(jnp.float32)
    return (weight * (by_row + by_col - 2.0 * pos_hit)).astype(jnp.bfloat16)


def per_device(ring, src_emb, tgt_emb, slot_group, counts, align, pair_weight):
    lang_size = lax.axis_size("lang")
    data_size = lax.axis_size("dp")
    row_count, emb_width = src_emb.shape
    per_slot = tgt_emb.shape[1]
    pair_rows = row_count * data_size
    inv_root = 1.0 / math.sqrt(emb_width)
    group_index = lax.axis_index("lang")
    shard_index = lax.axis_index("dp")
    slot_ids = jnp.arange(lang_size, dtype=jnp.int32)
    slot_of_group = jnp.zeros((lang_size,), jnp.int32).at[slot_group].set(slot_ids)
    ordered = tgt_emb[slot_of_group]
    arrived = lax.all_to_all(ordered, "lang", split_axis=0, concat_axis=1, tiled=True)
    partner = arrived[0]
    live_count = counts[group_index]
    weight = pair_weight[group_index]
    pair_align = align[0]
    all_rows = jnp.arange(pair_rows, dtype=jnp.int32)
    row_live = all_rows < live_count
    perm = target_index(pair_rows, row_count, per_slot, data_size)
    live_pos = (perm[None, :] == pair_align[:, None]) & row_live[:, None]
    col_live = jnp.max(live_pos.astype(jnp.int32), axis=0) > 0
    x_all = ring_gather(src_emb, ring)
    y_all = ring_gather(partner, ring)

    block = max(1, min(pair_rows, BLOCK_BYTES // (4 * pair_rows)))
    steps = pair_rows // block
    if steps == 1:
        is_pos = perm[None, :] == pair_align[:, None]
        scores_f = scores_of(x_all, y_all, is_pos, inv_root)
        row_lse, pos_score, col_max, col_sum = block_stats(scores_f, is_pos, row_live, col_live)
    else:
        def one_block(k, carry):
            row_lse, pos_score, col_max, col_sum = carry
            start = k * block
            x_blk = lax.dynamic_slice_in_dim(x_all, start, block)
            a_blk = lax.dynamic_slice_in_dim(pair_align, start, block)
            r_blk = lax.dynamic_slice_in_dim(row_live, start, block)
            is_pos = perm[None, :] == a_blk[:, None]
            s_blk = scores_of(x_blk, y_all, is_pos, inv_root)
            b_lse, b_pos, b_max, b_sum = block_stats(s_blk, is_pos, r_blk, col_live)
            top = jnp.maximum(col_max, b_max)
            col_sum = col_sum * jnp.exp(col_max - top) + b_sum * jnp.exp(b_max - top)
            row_lse = lax.dynamic_update_slice_in_dim(row_lse, b_lse, start, 0)
            pos_score = lax.dynamic_update_slice_in_dim(pos_score, b_pos, start, 0)
            return row_lse, pos_score, top, col_sum

        zeros = jnp.zeros((pair_rows,), jnp.float32)
        init = (zeros, zeros, jnp.full((pair_rows,), LOW_FILL, jnp.float32), zeros)
        row_lse, pos_score, col_max, col_sum = lax.fori_loop(0, steps, one_block, init)
    col_lse = col_max + jnp.log(col_sum + (1.0 - col_live.astype(jnp.float32)))

    row_f = row_live.astype(jnp.float32)
    col_f = col_live.astype(jnp.float32)
    total = jnp.sum(row_f * (row_lse - 2.0 * pos_score)) + jnp.sum(col_f * col_lse)
    pair_loss = (total / live_count.astype(jnp.float32)).reshape(1)

    mine = shard_index * row_count
    a_my = lax.dynamic_slice_in_dim(pair_align, mine, row_count)
    r_my = lax.dynamic_slice_in_dim(row_live, mine, row_count)
    lse_my = lax.dynamic_slice_in_dim(row_lse, mine, row_count)
    pos_rows = perm[None, :] == a_my[:, None]
    s_rows = scores_of(src_emb, y_all, pos_rows, inv_root)
    g_rows = grad_of(s_rows, pos_rows, r_my, col_live, lse_my, col_lse, weight)
    grad_src = (
        jnp.dot(g_rows, y_all, preferred_element_type=jnp.float32) * inv_root
    ).astype(jnp.bfloat16)

    p_my = lax.dynamic_slice_in_dim(perm, mine, row_count)
    c_my = lax.dynamic_slice_in_dim(col_live, mine, row_count)
    clse_my = lax.dynamic_slice_in_dim(col_lse, mine, row_count)
    pos_cols = p_my[None, :] == pair_align[:, None]
    s_cols = scores_of(x_all, partner, pos_cols, inv_root)
    g_cols = grad_of(s_cols, pos_cols, row_live, c_my, row_lse, clse_my, weight)
    own_terms = lax.dot_general(
        g_cols, x_all, (((0,), (0,)), ((), ())), preferred_element_type=jnp.float32
    )
    grad_local = (own_terms * inv_root).astype(jnp.bfloat16)
    returned = lax.all_to_all(
        grad_local.reshape(lang_size, per_slot, emb_width), "lang", split_axis=0, concat_axis=0, tiled=True
    )
    grad_tgt = returned[slot_group]
    return (grad_src, grad_tgt, pair_loss)


def solution(mesh):
    in_specs = (
        P(("lang", "dp"), None),
        P(None, ("lang", "dp"), None),
        P(),
        P(),
        P("lang", None),
        P(),
    )
    out_specs = (P(("lang", "dp"), None), P(None, ("lang", "dp"), None), P("lang"))
    return jax.shard_map(
        functools.partial(per_device, snake_ring(mesh)), mesh=mesh, in_specs=in_specs, out_specs=out_specs, check_vma=False
    )
```

```python
import functools
import math

import jax
import jax.numpy as jnp
from jax import lax
from jax.sharding import PartitionSpec as P

MARGIN = 0.3
LOW_FILL = -1e30
BLOCK_BYTES = 8 * 1024 * 1024


def target_index(col_count, row_count, per_slot, data_size):
    position = jnp.arange(col_count, dtype=jnp.int32)
    source = position // row_count
    within = position % row_count
    return (within // per_slot * data_size + source) * per_slot + within % per_slot


def snake_ring(mesh):
    count = mesh.shape["dp"]
    try:
        spots = [tuple(dev.coords) for dev in mesh.devices.reshape(-1, count)[0]]
    except (AttributeError, TypeError):
        return list(range(count))
    ys = sorted({s[1] for s in spots})
    zs = sorted({s[2] for s in spots})
    where = {(s[1], s[2]): d for d, s in enumerate(spots)}
    if len(where) != count or len(ys) * len(zs) != count:
        return list(range(count))
    rows, cols = (ys, zs) if len(ys) % 2 == 0 else (zs, ys)
    at = lambda r, c: where[(r, c) if rows is ys else (c, r)]
    if len(rows) == 1 or len(cols) == 1:
        return [at(r, c) for r in rows for c in cols]
    order = [at(rows[0], cols[0])]
    for k, r in enumerate(rows):
        seq = cols[1:] if k % 2 == 0 else cols[:0:-1]
        order += [at(r, c) for c in seq]
    order += [at(r, cols[0]) for r in rows[:0:-1]]
    return order


def slot_rows(tgt_emb, slot_group, group):
    rows = tgt_emb[0]
    for s in range(1, tgt_emb.shape[0]):
        rows = jnp.where(slot_group[s] == group, tgt_emb[s], rows)
    return rows


def ring_gather(block, ring):
    count = len(ring)
    place = [0] * count
    for p, d in enumerate(ring):
        place[d] = p
    ring_arr = jnp.array(ring, jnp.int32)
    my_dp = lax.axis_index("dp")
    my_pos = jnp.array(place, jnp.int32)[my_dp]
    ahead = [(ring[p], ring[(p + 1) % count]) for p in range(count)]
    behind = [(ring[p], ring[(p - 1) % count]) for p in range(count)]
    rows = block.shape[0]
    out = jnp.zeros((count * rows,) + block.shape[1:], block.dtype)
    out = lax.dynamic_update_slice_in_dim(out, block, my_dp * rows, 0)
    for pairs, steps, sign in ((ahead, count // 2, -1), (behind, count - 1 - count // 2, 1)):
        cur = block
        for t in range(1, steps + 1):
            cur = lax.ppermute(cur, "dp", pairs)
            origin = ring_arr[(my_pos + sign * t) % count]
            out = lax.dynamic_update_slice_in_dim(out, cur, origin * rows, 0)
    return out


def scores_of(x_rows, y_rows, pos_mask, inv_root):
    raw_dot = lax.dot_general(
        x_rows, y_rows, (((1,), (1,)), ((), ())), preferred_element_type=jnp.float32
    )
    return raw_dot * inv_root - MARGIN * pos_mask.astype(jnp.float32)


def block_stats(scores_f, is_pos, row_live, col_ok):
    row_max = jnp.max(jnp.where(col_ok[None, :], scores_f, LOW_FILL), axis=1)
    row_sum = jnp.sum(
        jnp.where(col_ok[None, :], jnp.exp(scores_f - row_max[:, None]), 0.0), axis=1
    )
    row_lse = row_max + jnp.log(row_sum + (1.0 - row_live.astype(jnp.float32)))
    pos_score = jnp.sum(jnp.where(is_pos, scores_f, 0.0), axis=1)
    col_max = jnp.max(jnp.where(row_live[:, None], scores_f, LOW_FILL), axis=0)
    col_sum = jnp.sum(
        jnp.where(row_live[:, None], jnp.exp(scores_f - col_max[None, :]), 0.0), axis=0
    )
    return row_lse, pos_score, col_max, col_sum


def grad_of(scores_f, is_pos, row_ok, col_ok, row_lse, col_lse, weight):
    both_live = row_ok[:, None] & col_ok[None, :]
    by_row = jnp.where(both_live, jnp.exp(scores_f - row_lse[:, None]), 0.0)
    by_col = jnp.where(both_live, jnp.exp(scores_f - col_lse[None, :]), 0.0)
    pos_hit = (is_pos & row_ok[:, None]).astype(jnp.float32)
    return (weight * (by_row + by_col - 2.0 * pos_hit)).astype(jnp.bfloat16)


def per_device(ring, src_emb, tgt_emb, slot_group, counts, align, pair_weight):
    lang_size = lax.axis_size("lang")
    data_size = lax.axis_size("dp")
    row_count, emb_width = src_emb.shape
    per_slot = tgt_emb.shape[1]
    pair_rows = row_count * data_size
    inv_root = 1.0 / math.sqrt(emb_width)
    group_index = lax.axis_index("lang")
    shard_index = lax.axis_index("dp")
    slot_ids = jnp.arange(lang_size, dtype=jnp.int32)
    slot_of_group = jnp.zeros((lang_size,), jnp.int32).at[slot_group].set(slot_ids)
    ordered = tgt_emb[slot_of_group]
    arrived = lax.all_to_all(ordered, "lang", split_axis=0, concat_axis=1, tiled=True)
    partner = arrived[0]
    live_count = counts[group_index]
    weight = pair_weight[group_index]
    pair_align = align[0]
    all_rows = jnp.arange(pair_rows, dtype=jnp.int32)
    row_live = all_rows < live_count
    perm = target_index(pair_rows, row_count, per_slot, data_size)
    live_pos = (perm[None, :] == pair_align[:, None]) & row_live[:, None]
    col_live = jnp.max(live_pos.astype(jnp.int32), axis=0) > 0
    x_all = ring_gather(src_emb, ring)
    y_all = ring_gather(partner, ring)

    block = max(1, min(pair_rows, BLOCK_BYTES // (4 * pair_rows)))
    steps = pair_rows // block
    if steps == 1:
        is_pos = perm[None, :] == pair_align[:, None]
        scores_f = scores_of(x_all, y_all, is_pos, inv_root)
        row_lse, pos_score, col_max, col_sum = block_stats(scores_f, is_pos, row_live, col_live)
    else:
        def one_block(k, carry):
            row_lse, pos_score, col_max, col_sum = carry
            start = k * block
            x_blk = lax.dynamic_slice_in_dim(x_all, start, block)
            a_blk = lax.dynamic_slice_in_dim(pair_align, start, block)
            r_blk = lax.dynamic_slice_in_dim(row_live, start, block)
            is_pos = perm[None, :] == a_blk[:, None]
            s_blk = scores_of(x_blk, y_all, is_pos, inv_root)
            b_lse, b_pos, b_max, b_sum = block_stats(s_blk, is_pos, r_blk, col_live)
            top = jnp.maximum(col_max, b_max)
            col_sum = col_sum * jnp.exp(col_max - top) + b_sum * jnp.exp(b_max - top)
            row_lse = lax.dynamic_update_slice_in_dim(row_lse, b_lse, start, 0)
            pos_score = lax.dynamic_update_slice_in_dim(pos_score, b_pos, start, 0)
            return row_lse, pos_score, top, col_sum

        zeros = jnp.zeros((pair_rows,), jnp.float32)
        init = (zeros, zeros, jnp.full((pair_rows,), LOW_FILL, jnp.float32), zeros)
        row_lse, pos_score, col_max, col_sum = lax.fori_loop(0, steps, one_block, init)
    col_lse = col_max + jnp.log(col_sum + (1.0 - col_live.astype(jnp.float32)))

    row_f = row_live.astype(jnp.float32)
    col_f = col_live.astype(jnp.float32)
    total = jnp.sum(row_f * (row_lse - 2.0 * pos_score)) + jnp.sum(col_f * col_lse)
    pair_loss = (total / live_count.astype(jnp.float32)).reshape(1)

    mine = shard_index * row_count
    a_my = lax.dynamic_slice_in_dim(pair_align, mine, row_count)
    r_my = lax.dynamic_slice_in_dim(row_live, mine, row_count)
    lse_my = lax.dynamic_slice_in_dim(row_lse, mine, row_count)
    pos_rows = perm[None, :] == a_my[:, None]
    s_rows = scores_of(src_emb, y_all, pos_rows, inv_root)
    g_rows = grad_of(s_rows, pos_rows, r_my, col_live, lse_my, col_lse, weight)
    grad_src = (
        jnp.dot(g_rows, y_all, preferred_element_type=jnp.float32) * inv_root
    ).astype(jnp.bfloat16)

    p_my = lax.dynamic_slice_in_dim(perm, mine, row_count)
    c_my = lax.dynamic_slice_in_dim(col_live, mine, row_count)
    clse_my = lax.dynamic_slice_in_dim(col_lse, mine, row_count)
    pos_cols = p_my[None, :] == pair_align[:, None]
    s_cols = scores_of(x_all, partner, pos_cols, inv_root)
    g_cols = grad_of(s_cols, pos_cols, row_live, c_my, row_lse, clse_my, weight)
    own_terms = lax.dot_general(
        g_cols, x_all, (((0,), (0,)), ((), ())), preferred_element_type=jnp.float32
    )
    grad_local = (own_terms * inv_root).astype(jnp.bfloat16)
    returned = jnp.zeros((lang_size, per_slot, emb_width), grad_local.dtype)
    kept = lax.dynamic_slice_in_dim(grad_local, group_index * per_slot, per_slot)
    returned = lax.dynamic_update_index_in_dim(returned, kept, group_index, 0)
    for k in range(1, lang_size):
        dest = (group_index + k) % lang_size
        sent = lax.dynamic_slice_in_dim(grad_local, dest * per_slot, per_slot)
        got = lax.ppermute(sent, "lang", [(l, (l + k) % lang_size) for l in range(lang_size)])
        returned = lax.dynamic_update_index_in_dim(returned, got, (group_index - k) % lang_size, 0)
    group_ids = jnp.arange(lang_size, dtype=jnp.int32)
    grad_tgt = jnp.stack([slot_rows(returned, group_ids, slot_group[s]) for s in range(lang_size)])
    return (grad_src, grad_tgt, pair_loss)


def solution(mesh):
    in_specs = (
        P(("lang", "dp"), None),
        P(None, ("lang", "dp"), None),
        P(),
        P(),
        P("lang", None),
        P(),
    )
    out_specs = (P(("lang", "dp"), None), P(None, ("lang", "dp"), None), P("lang"))
    return jax.shard_map(
        functools.partial(per_device, snake_ring(mesh)), mesh=mesh, in_specs=in_specs, out_specs=out_specs, check_vma=False
    )
```

```python
import functools
import math

import jax
import jax.numpy as jnp
from jax import lax
from jax.sharding import PartitionSpec as P

MARGIN = 0.3
LOW_FILL = -1e30
BLOCK_BYTES = 8 * 1024 * 1024


def target_index(col_count, row_count, per_slot, data_size):
    position = jnp.arange(col_count, dtype=jnp.int32)
    source = position // row_count
    within = position % row_count
    return (within // per_slot * data_size + source) * per_slot + within % per_slot


def snake_ring(mesh):
    count = mesh.shape["dp"]
    try:
        spots = [tuple(dev.coords) for dev in mesh.devices.reshape(-1, count)[0]]
    except (AttributeError, TypeError):
        return list(range(count))
    ys = sorted({s[1] for s in spots})
    zs = sorted({s[2] for s in spots})
    where = {(s[1], s[2]): d for d, s in enumerate(spots)}
    if len(where) != count or len(ys) * len(zs) != count:
        return list(range(count))
    rows, cols = (ys, zs) if len(ys) % 2 == 0 else (zs, ys)
    at = lambda r, c: where[(r, c) if rows is ys else (c, r)]
    if len(rows) == 1 or len(cols) == 1:
        return [at(r, c) for r in rows for c in cols]
    order = [at(rows[0], cols[0])]
    for k, r in enumerate(rows):
        seq = cols[1:] if k % 2 == 0 else cols[:0:-1]
        order += [at(r, c) for c in seq]
    order += [at(r, cols[0]) for r in rows[:0:-1]]
    return order


def ring_gather(block, ring):
    count = len(ring)
    place = [0] * count
    for p, d in enumerate(ring):
        place[d] = p
    ring_arr = jnp.array(ring, jnp.int32)
    my_dp = lax.axis_index("dp")
    my_pos = jnp.array(place, jnp.int32)[my_dp]
    ahead = [(ring[p], ring[(p + 1) % count]) for p in range(count)]
    behind = [(ring[p], ring[(p - 1) % count]) for p in range(count)]
    rows = block.shape[0]
    out = jnp.zeros((count * rows,) + block.shape[1:], block.dtype)
    out = lax.dynamic_update_slice_in_dim(out, block, my_dp * rows, 0)
    for pairs, steps, sign in ((ahead, count // 2, -1), (behind, count - 1 - count // 2, 1)):
        cur = block
        for t in range(1, steps + 1):
            cur = lax.ppermute(cur, "dp", pairs)
            origin = ring_arr[(my_pos + sign * t) % count]
            out = lax.dynamic_update_slice_in_dim(out, cur, origin * rows, 0)
    return out


def scores_of(x_rows, y_rows, pos_mask, inv_root):
    raw_dot = lax.dot_general(
        x_rows, y_rows, (((1,), (1,)), ((), ())), preferred_element_type=jnp.float32
    )
    return raw_dot * inv_root - MARGIN * pos_mask.astype(jnp.float32)


def block_stats(scores_f, is_pos, row_live, col_ok):
    row_max = jnp.max(jnp.where(col_ok[None, :], scores_f, LOW_FILL), axis=1)
    row_sum = jnp.sum(
        jnp.where(col_ok[None, :], jnp.exp(scores_f - row_max[:, None]), 0.0), axis=1
    )
    row_lse = row_max + jnp.log(row_sum + (1.0 - row_live.astype(jnp.float32)))
    pos_score = jnp.sum(jnp.where(is_pos, scores_f, 0.0), axis=1)
    col_max = jnp.max(jnp.where(row_live[:, None], scores_f, LOW_FILL), axis=0)
    col_sum = jnp.sum(
        jnp.where(row_live[:, None], jnp.exp(scores_f - col_max[None, :]), 0.0), axis=0
    )
    return row_lse, pos_score, col_max, col_sum


def grad_of(scores_f, is_pos, row_ok, col_ok, row_lse, col_lse, weight):
    both_live = row_ok[:, None] & col_ok[None, :]
    by_row = jnp.where(both_live, jnp.exp(scores_f - row_lse[:, None]), 0.0)
    by_col = jnp.where(both_live, jnp.exp(scores_f - col_lse[None, :]), 0.0)
    pos_hit = (is_pos & row_ok[:, None]).astype(jnp.float32)
    return (weight * (by_row + by_col - 2.0 * pos_hit)).astype(jnp.bfloat16)


def per_device(ring, src_emb, tgt_emb, slot_group, counts, align, pair_weight):
    lang_size = lax.axis_size("lang")
    data_size = lax.axis_size("dp")
    row_count, emb_width = src_emb.shape
    per_slot = tgt_emb.shape[1]
    pair_rows = row_count * data_size
    inv_root = 1.0 / math.sqrt(emb_width)
    group_index = lax.axis_index("lang")
    shard_index = lax.axis_index("dp")
    slot_ids = jnp.arange(lang_size, dtype=jnp.int32)
    slot_of_group = jnp.zeros((lang_size,), jnp.int32).at[slot_group].set(slot_ids)
    ordered = tgt_emb[slot_of_group]
    arrived = lax.all_to_all(ordered, "lang", split_axis=0, concat_axis=1, tiled=True)
    partner = arrived[0]
    live_count = counts[group_index]
    weight = pair_weight[group_index]
    pair_align = align[0]
    all_rows = jnp.arange(pair_rows, dtype=jnp.int32)
    row_live = all_rows < live_count
    perm = target_index(pair_rows, row_count, per_slot, data_size)
    live_pos = (perm[None, :] == pair_align[:, None]) & row_live[:, None]
    col_live = jnp.max(live_pos.astype(jnp.int32), axis=0) > 0
    after = src_emb + jnp.zeros_like(src_emb) * partner[:1, :1]
    x_all = ring_gather(after, ring)
    y_all = ring_gather(partner, ring)

    block = max(1, min(pair_rows, BLOCK_BYTES // (4 * pair_rows)))
    steps = pair_rows // block
    if steps == 1:
        is_pos = perm[None, :] == pair_align[:, None]
        scores_f = scores_of(x_all, y_all, is_pos, inv_root)
        row_lse, pos_score, col_max, col_sum = block_stats(scores_f, is_pos, row_live, col_live)
    else:
        def one_block(k, carry):
            row_lse, pos_score, col_max, col_sum = carry
            start = k * block
            x_blk = lax.dynamic_slice_in_dim(x_all, start, block)
            a_blk = lax.dynamic_slice_in_dim(pair_align, start, block)
            r_blk = lax.dynamic_slice_in_dim(row_live, start, block)
            is_pos = perm[None, :] == a_blk[:, None]
            s_blk = scores_of(x_blk, y_all, is_pos, inv_root)
            b_lse, b_pos, b_max, b_sum = block_stats(s_blk, is_pos, r_blk, col_live)
            top = jnp.maximum(col_max, b_max)
            col_sum = col_sum * jnp.exp(col_max - top) + b_sum * jnp.exp(b_max - top)
            row_lse = lax.dynamic_update_slice_in_dim(row_lse, b_lse, start, 0)
            pos_score = lax.dynamic_update_slice_in_dim(pos_score, b_pos, start, 0)
            return row_lse, pos_score, top, col_sum

        zeros = jnp.zeros((pair_rows,), jnp.float32)
        init = (zeros, zeros, jnp.full((pair_rows,), LOW_FILL, jnp.float32), zeros)
        row_lse, pos_score, col_max, col_sum = lax.fori_loop(0, steps, one_block, init)
    col_lse = col_max + jnp.log(col_sum + (1.0 - col_live.astype(jnp.float32)))

    row_f = row_live.astype(jnp.float32)
    col_f = col_live.astype(jnp.float32)
    total = jnp.sum(row_f * (row_lse - 2.0 * pos_score)) + jnp.sum(col_f * col_lse)
    pair_loss = (total / live_count.astype(jnp.float32)).reshape(1)

    mine = shard_index * row_count
    a_my = lax.dynamic_slice_in_dim(pair_align, mine, row_count)
    r_my = lax.dynamic_slice_in_dim(row_live, mine, row_count)
    lse_my = lax.dynamic_slice_in_dim(row_lse, mine, row_count)
    pos_rows = perm[None, :] == a_my[:, None]
    s_rows = scores_of(src_emb, y_all, pos_rows, inv_root)
    g_rows = grad_of(s_rows, pos_rows, r_my, col_live, lse_my, col_lse, weight)
    grad_src = (
        jnp.dot(g_rows, y_all, preferred_element_type=jnp.float32) * inv_root
    ).astype(jnp.bfloat16)

    p_my = lax.dynamic_slice_in_dim(perm, mine, row_count)
    c_my = lax.dynamic_slice_in_dim(col_live, mine, row_count)
    clse_my = lax.dynamic_slice_in_dim(col_lse, mine, row_count)
    pos_cols = p_my[None, :] == pair_align[:, None]
    s_cols = scores_of(x_all, partner, pos_cols, inv_root)
    g_cols = grad_of(s_cols, pos_cols, row_live, c_my, row_lse, clse_my, weight)
    own_terms = lax.dot_general(
        g_cols, x_all, (((0,), (0,)), ((), ())), preferred_element_type=jnp.float32
    )
    grad_local = (own_terms * inv_root).astype(jnp.bfloat16)
    returned = lax.all_to_all(
        grad_local.reshape(lang_size, per_slot, emb_width), "lang", split_axis=0, concat_axis=0, tiled=True
    )
    grad_tgt = returned[slot_group]
    return (grad_src, grad_tgt, pair_loss)


def solution(mesh):
    in_specs = (
        P(("lang", "dp"), None),
        P(None, ("lang", "dp"), None),
        P(),
        P(),
        P("lang", None),
        P(),
    )
    out_specs = (P(("lang", "dp"), None), P(None, ("lang", "dp"), None), P("lang"))
    return jax.shard_map(
        functools.partial(per_device, snake_ring(mesh)), mesh=mesh, in_specs=in_specs, out_specs=out_specs, check_vma=False
    )
```

```python
import functools
import math

import jax
import jax.numpy as jnp
from jax import lax
from jax.sharding import PartitionSpec as P

MARGIN = 0.3
LOW_FILL = -1e30
BLOCK_BYTES = 8 * 1024 * 1024


def target_index(col_count, row_count, per_slot, data_size):
    position = jnp.arange(col_count, dtype=jnp.int32)
    source = position // row_count
    within = position % row_count
    return (within // per_slot * data_size + source) * per_slot + within % per_slot


def snake_ring(mesh):
    count = mesh.shape["dp"]
    try:
        spots = [tuple(dev.coords) for dev in mesh.devices.reshape(-1, count)[0]]
    except (AttributeError, TypeError):
        return list(range(count))
    ys = sorted({s[1] for s in spots})
    zs = sorted({s[2] for s in spots})
    where = {(s[1], s[2]): d for d, s in enumerate(spots)}
    if len(where) != count or len(ys) * len(zs) != count:
        return list(range(count))
    rows, cols = (ys, zs) if len(ys) % 2 == 0 else (zs, ys)
    at = lambda r, c: where[(r, c) if rows is ys else (c, r)]
    if len(rows) == 1 or len(cols) == 1:
        return [at(r, c) for r in rows for c in cols]
    order = [at(rows[0], cols[0])]
    for k, r in enumerate(rows):
        seq = cols[1:] if k % 2 == 0 else cols[:0:-1]
        order += [at(r, c) for c in seq]
    order += [at(r, cols[0]) for r in rows[:0:-1]]
    return order


def ring_gather(block, ring, lang_size):
    count = len(ring)
    place = [0] * count
    for p, d in enumerate(ring):
        place[d] = p
    ring_arr = jnp.array(ring, jnp.int32)
    my_dp = lax.axis_index("dp")
    my_pos = jnp.array(place, jnp.int32)[my_dp]
    mirror = 1 - 2 * (lax.axis_index("lang") % 2)

    def pairs_for(even_step):
        out = []
        for l in range(lang_size):
            step = even_step if l % 2 == 0 else -even_step
            out += [(l * count + ring[p], l * count + ring[(p + step) % count]) for p in range(count)]
        return out

    rows = block.shape[0]
    out = jnp.zeros((count * rows,) + block.shape[1:], block.dtype)
    out = lax.dynamic_update_slice_in_dim(out, block, my_dp * rows, 0)
    for even_step, steps in ((1, count // 2), (-1, count - 1 - count // 2)):
        pairs = pairs_for(even_step)
        cur = block
        for t in range(1, steps + 1):
            cur = lax.ppermute(cur, ("lang", "dp"), pairs)
            origin = ring_arr[(my_pos - even_step * mirror * t) % count]
            out = lax.dynamic_update_slice_in_dim(out, cur, origin * rows, 0)
    return out


def scores_of(x_rows, y_rows, pos_mask, inv_root):
    raw_dot = lax.dot_general(
        x_rows, y_rows, (((1,), (1,)), ((), ())), preferred_element_type=jnp.float32
    )
    return raw_dot * inv_root - MARGIN * pos_mask.astype(jnp.float32)


def block_stats(scores_f, is_pos, row_live, col_ok):
    row_max = jnp.max(jnp.where(col_ok[None, :], scores_f, LOW_FILL), axis=1)
    row_sum = jnp.sum(
        jnp.where(col_ok[None, :], jnp.exp(scores_f - row_max[:, None]), 0.0), axis=1
    )
    row_lse = row_max + jnp.log(row_sum + (1.0 - row_live.astype(jnp.float32)))
    pos_score = jnp.sum(jnp.where(is_pos, scores_f, 0.0), axis=1)
    col_max = jnp.max(jnp.where(row_live[:, None], scores_f, LOW_FILL), axis=0)
    col_sum = jnp.sum(
        jnp.where(row_live[:, None], jnp.exp(scores_f - col_max[None, :]), 0.0), axis=0
    )
    return row_lse, pos_score, col_max, col_sum


def grad_of(scores_f, is_pos, row_ok, col_ok, row_lse, col_lse, weight):
    both_live = row_ok[:, None] & col_ok[None, :]
    by_row = jnp.where(both_live, jnp.exp(scores_f - row_lse[:, None]), 0.0)
    by_col = jnp.where(both_live, jnp.exp(scores_f - col_lse[None, :]), 0.0)
    pos_hit = (is_pos & row_ok[:, None]).astype(jnp.float32)
    return (weight * (by_row + by_col - 2.0 * pos_hit)).astype(jnp.bfloat16)


def per_device(ring, src_emb, tgt_emb, slot_group, counts, align, pair_weight):
    lang_size = lax.axis_size("lang")
    data_size = lax.axis_size("dp")
    row_count, emb_width = src_emb.shape
    per_slot = tgt_emb.shape[1]
    pair_rows = row_count * data_size
    inv_root = 1.0 / math.sqrt(emb_width)
    group_index = lax.axis_index("lang")
    shard_index = lax.axis_index("dp")
    slot_ids = jnp.arange(lang_size, dtype=jnp.int32)
    slot_of_group = jnp.zeros((lang_size,), jnp.int32).at[slot_group].set(slot_ids)
    ordered = tgt_emb[slot_of_group]
    arrived = lax.all_to_all(ordered, "lang", split_axis=0, concat_axis=1, tiled=True)
    partner = arrived[0]
    live_count = counts[group_index]
    weight = pair_weight[group_index]
    pair_align = align[0]
    all_rows = jnp.arange(pair_rows, dtype=jnp.int32)
    row_live = all_rows < live_count
    perm = target_index(pair_rows, row_count, per_slot, data_size)
    live_pos = (perm[None, :] == pair_align[:, None]) & row_live[:, None]
    col_live = jnp.max(live_pos.astype(jnp.int32), axis=0) > 0
    x_all = ring_gather(src_emb, ring, lang_size)
    y_all = ring_gather(partner, ring, lang_size)

    block = max(1, min(pair_rows, BLOCK_BYTES // (4 * pair_rows)))
    steps = pair_rows // block
    if steps == 1:
        is_pos = perm[None, :] == pair_align[:, None]
        scores_f = scores_of(x_all, y_all, is_pos, inv_root)
        row_lse, pos_score, col_max, col_sum = block_stats(scores_f, is_pos, row_live, col_live)
    else:
        def one_block(k, carry):
            row_lse, pos_score, col_max, col_sum = carry
            start = k * block
            x_blk = lax.dynamic_slice_in_dim(x_all, start, block)
            a_blk = lax.dynamic_slice_in_dim(pair_align, start, block)
            r_blk = lax.dynamic_slice_in_dim(row_live, start, block)
            is_pos = perm[None, :] == a_blk[:, None]
            s_blk = scores_of(x_blk, y_all, is_pos, inv_root)
            b_lse, b_pos, b_max, b_sum = block_stats(s_blk, is_pos, r_blk, col_live)
            top = jnp.maximum(col_max, b_max)
            col_sum = col_sum * jnp.exp(col_max - top) + b_sum * jnp.exp(b_max - top)
            row_lse = lax.dynamic_update_slice_in_dim(row_lse, b_lse, start, 0)
            pos_score = lax.dynamic_update_slice_in_dim(pos_score, b_pos, start, 0)
            return row_lse, pos_score, top, col_sum

        zeros = jnp.zeros((pair_rows,), jnp.float32)
        init = (zeros, zeros, jnp.full((pair_rows,), LOW_FILL, jnp.float32), zeros)
        row_lse, pos_score, col_max, col_sum = lax.fori_loop(0, steps, one_block, init)
    col_lse = col_max + jnp.log(col_sum + (1.0 - col_live.astype(jnp.float32)))

    row_f = row_live.astype(jnp.float32)
    col_f = col_live.astype(jnp.float32)
    total = jnp.sum(row_f * (row_lse - 2.0 * pos_score)) + jnp.sum(col_f * col_lse)
    pair_loss = (total / live_count.astype(jnp.float32)).reshape(1)

    mine = shard_index * row_count
    a_my = lax.dynamic_slice_in_dim(pair_align, mine, row_count)
    r_my = lax.dynamic_slice_in_dim(row_live, mine, row_count)
    lse_my = lax.dynamic_slice_in_dim(row_lse, mine, row_count)
    pos_rows = perm[None, :] == a_my[:, None]
    s_rows = scores_of(src_emb, y_all, pos_rows, inv_root)
    g_rows = grad_of(s_rows, pos_rows, r_my, col_live, lse_my, col_lse, weight)
    grad_src = (
        jnp.dot(g_rows, y_all, preferred_element_type=jnp.float32) * inv_root
    ).astype(jnp.bfloat16)

    p_my = lax.dynamic_slice_in_dim(perm, mine, row_count)
    c_my = lax.dynamic_slice_in_dim(col_live, mine, row_count)
    clse_my = lax.dynamic_slice_in_dim(col_lse, mine, row_count)
    pos_cols = p_my[None, :] == pair_align[:, None]
    s_cols = scores_of(x_all, partner, pos_cols, inv_root)
    g_cols = grad_of(s_cols, pos_cols, row_live, c_my, row_lse, clse_my, weight)
    own_terms = lax.dot_general(
        g_cols, x_all, (((0,), (0,)), ((), ())), preferred_element_type=jnp.float32
    )
    grad_local = (own_terms * inv_root).astype(jnp.bfloat16)
    returned = lax.all_to_all(
        grad_local.reshape(lang_size, per_slot, emb_width), "lang", split_axis=0, concat_axis=0, tiled=True
    )
    grad_tgt = returned[slot_group]
    return (grad_src, grad_tgt, pair_loss)


def solution(mesh):
    in_specs = (
        P(("lang", "dp"), None),
        P(None, ("lang", "dp"), None),
        P(),
        P(),
        P("lang", None),
        P(),
    )
    out_specs = (P(("lang", "dp"), None), P(None, ("lang", "dp"), None), P("lang"))
    return jax.shard_map(
        functools.partial(per_device, snake_ring(mesh)), mesh=mesh, in_specs=in_specs, out_specs=out_specs, check_vma=False
    )
```

```python
import functools
import math

import jax
import jax.numpy as jnp
from jax import lax
from jax.sharding import PartitionSpec as P

MARGIN = 0.3
LOW_FILL = -1e30
BLOCK_BYTES = 8 * 1024 * 1024


def target_index(col_count, row_count, per_slot, data_size):
    position = jnp.arange(col_count, dtype=jnp.int32)
    source = position // row_count
    within = position % row_count
    return (within // per_slot * data_size + source) * per_slot + within % per_slot


def snake_ring(mesh):
    count = mesh.shape["dp"]
    try:
        spots = [tuple(dev.coords) for dev in mesh.devices.reshape(-1, count)[0]]
    except (AttributeError, TypeError):
        return list(range(count))
    ys = sorted({s[1] for s in spots})
    zs = sorted({s[2] for s in spots})
    where = {(s[1], s[2]): d for d, s in enumerate(spots)}
    if len(where) != count or len(ys) * len(zs) != count:
        return list(range(count))
    rows, cols = (ys, zs) if len(ys) % 2 == 0 else (zs, ys)
    at = lambda r, c: where[(r, c) if rows is ys else (c, r)]
    if len(rows) == 1 or len(cols) == 1:
        return [at(r, c) for r in rows for c in cols]
    order = [at(rows[0], cols[0])]
    for k, r in enumerate(rows):
        seq = cols[1:] if k % 2 == 0 else cols[:0:-1]
        order += [at(r, c) for c in seq]
    order += [at(r, cols[0]) for r in rows[:0:-1]]
    return order


def ring_gather(block, ring, lang_size):
    count = len(ring)
    place = [0] * count
    for p, d in enumerate(ring):
        place[d] = p
    ring_arr = jnp.array(ring, jnp.int32)
    my_dp = lax.axis_index("dp")
    my_pos = jnp.array(place, jnp.int32)[my_dp]
    mirror = 1 - 2 * (lax.axis_index("lang") % 2)

    def pairs_for(even_step):
        out = []
        for l in range(lang_size):
            step = even_step if l % 2 == 0 else -even_step
            out += [(l * count + ring[p], l * count + ring[(p + step) % count]) for p in range(count)]
        return out

    rows = block.shape[0]
    out = jnp.zeros((count * rows,) + block.shape[1:], block.dtype)
    out = lax.dynamic_update_slice_in_dim(out, block, my_dp * rows, 0)
    arrivals = [(my_dp, block)]
    for even_step, steps in ((1, count // 2), (-1, count - 1 - count // 2)):
        pairs = pairs_for(even_step)
        cur = block
        for t in range(1, steps + 1):
            cur = lax.ppermute(cur, ("lang", "dp"), pairs)
            origin = ring_arr[(my_pos - even_step * mirror * t) % count]
            out = lax.dynamic_update_slice_in_dim(out, cur, origin * rows, 0)
            arrivals.append((origin, cur))
    return out, arrivals


def scores_of(x_rows, y_rows, pos_mask, inv_root):
    raw_dot = lax.dot_general(
        x_rows, y_rows, (((1,), (1,)), ((), ())), preferred_element_type=jnp.float32
    )
    return raw_dot * inv_root - MARGIN * pos_mask.astype(jnp.float32)


def block_stats(scores_f, is_pos, row_live, col_ok):
    row_max = jnp.max(jnp.where(col_ok[None, :], scores_f, LOW_FILL), axis=1)
    row_sum = jnp.sum(
        jnp.where(col_ok[None, :], jnp.exp(scores_f - row_max[:, None]), 0.0), axis=1
    )
    row_lse = row_max + jnp.log(row_sum + (1.0 - row_live.astype(jnp.float32)))
    pos_score = jnp.sum(jnp.where(is_pos, scores_f, 0.0), axis=1)
    col_max = jnp.max(jnp.where(row_live[:, None], scores_f, LOW_FILL), axis=0)
    col_sum = jnp.sum(
        jnp.where(row_live[:, None], jnp.exp(scores_f - col_max[None, :]), 0.0), axis=0
    )
    return row_lse, pos_score, col_max, col_sum


def grad_of(scores_f, is_pos, row_ok, col_ok, row_lse, col_lse, weight):
    both_live = row_ok[:, None] & col_ok[None, :]
    by_row = jnp.where(both_live, jnp.exp(scores_f - row_lse[:, None]), 0.0)
    by_col = jnp.where(both_live, jnp.exp(scores_f - col_lse[None, :]), 0.0)
    pos_hit = (is_pos & row_ok[:, None]).astype(jnp.float32)
    return (weight * (by_row + by_col - 2.0 * pos_hit)).astype(jnp.bfloat16)


def per_device(ring, src_emb, tgt_emb, slot_group, counts, align, pair_weight):
    lang_size = lax.axis_size("lang")
    data_size = lax.axis_size("dp")
    row_count, emb_width = src_emb.shape
    per_slot = tgt_emb.shape[1]
    pair_rows = row_count * data_size
    inv_root = 1.0 / math.sqrt(emb_width)
    group_index = lax.axis_index("lang")
    shard_index = lax.axis_index("dp")
    slot_ids = jnp.arange(lang_size, dtype=jnp.int32)
    slot_of_group = jnp.zeros((lang_size,), jnp.int32).at[slot_group].set(slot_ids)
    ordered = tgt_emb[slot_of_group]
    arrived = lax.all_to_all(ordered, "lang", split_axis=0, concat_axis=1, tiled=True)
    partner = arrived[0]
    live_count = counts[group_index]
    weight = pair_weight[group_index]
    pair_align = align[0]
    all_rows = jnp.arange(pair_rows, dtype=jnp.int32)
    row_live = all_rows < live_count
    perm = target_index(pair_rows, row_count, per_slot, data_size)
    live_pos = (perm[None, :] == pair_align[:, None]) & row_live[:, None]
    col_live = jnp.max(live_pos.astype(jnp.int32), axis=0) > 0
    x_all, _ = ring_gather(src_emb, ring, lang_size)
    y_all, y_arrivals = ring_gather(partner, ring, lang_size)

    if pair_rows * pair_rows * 4 <= BLOCK_BYTES:
        row_f = row_live.astype(jnp.float32)
        within = jnp.arange(row_count, dtype=jnp.int32)
        run_max = jnp.full((pair_rows,), LOW_FILL, jnp.float32)
        run_sum = jnp.zeros((pair_rows,), jnp.float32)
        pos_score = jnp.zeros((pair_rows,), jnp.float32)
        col_lse = jnp.zeros((pair_rows,), jnp.float32)
        col_term = jnp.float32(0.0)
        for origin, y_blk in y_arrivals:
            perm_blk = (within // per_slot * data_size + origin) * per_slot + within % per_slot
            pos_blk = perm_blk[None, :] == pair_align[:, None]
            live_blk = jnp.max((pos_blk & row_live[:, None]).astype(jnp.int32), axis=0) > 0
            s_blk = scores_of(x_all, y_blk, pos_blk, inv_root)
            b_max = jnp.max(jnp.where(row_live[:, None], s_blk, LOW_FILL), axis=0)
            b_sum = jnp.sum(jnp.where(row_live[:, None], jnp.exp(s_blk - b_max[None, :]), 0.0), axis=0)
            b_lse = b_max + jnp.log(b_sum + (1.0 - live_blk.astype(jnp.float32)))
            col_lse = lax.dynamic_update_slice_in_dim(col_lse, b_lse, origin * row_count, 0)
            col_term = col_term + jnp.sum(live_blk.astype(jnp.float32) * b_lse)
            r_max = jnp.max(jnp.where(live_blk[None, :], s_blk, LOW_FILL), axis=1)
            top = jnp.maximum(run_max, r_max)
            r_sum = jnp.sum(jnp.where(live_blk[None, :], jnp.exp(s_blk - top[:, None]), 0.0), axis=1)
            run_sum = run_sum * jnp.exp(run_max - top) + r_sum
            run_max = top
            pos_score = pos_score + jnp.sum(jnp.where(pos_blk, s_blk, 0.0), axis=1)
        row_lse = run_max + jnp.log(run_sum + (1.0 - row_f))
    else:
        block = max(1, min(pair_rows, BLOCK_BYTES // (4 * pair_rows)))
        steps = pair_rows // block
        if steps == 1:
            is_pos = perm[None, :] == pair_align[:, None]
            scores_f = scores_of(x_all, y_all, is_pos, inv_root)
            row_lse, pos_score, col_max, col_sum = block_stats(scores_f, is_pos, row_live, col_live)
        else:
            def one_block(k, carry):
                row_lse, pos_score, col_max, col_sum = carry
                start = k * block
                x_blk = lax.dynamic_slice_in_dim(x_all, start, block)
                a_blk = lax.dynamic_slice_in_dim(pair_align, start, block)
                r_blk = lax.dynamic_slice_in_dim(row_live, start, block)
                is_pos = perm[None, :] == a_blk[:, None]
                s_blk = scores_of(x_blk, y_all, is_pos, inv_root)
                b_lse, b_pos, b_max, b_sum = block_stats(s_blk, is_pos, r_blk, col_live)
                top = jnp.maximum(col_max, b_max)
                col_sum = col_sum * jnp.exp(col_max - top) + b_sum * jnp.exp(b_max - top)
                row_lse = lax.dynamic_update_slice_in_dim(row_lse, b_lse, start, 0)
                pos_score = lax.dynamic_update_slice_in_dim(pos_score, b_pos, start, 0)
                return row_lse, pos_score, top, col_sum

            zeros = jnp.zeros((pair_rows,), jnp.float32)
            init = (zeros, zeros, jnp.full((pair_rows,), LOW_FILL, jnp.float32), zeros)
            row_lse, pos_score, col_max, col_sum = lax.fori_loop(0, steps, one_block, init)
        col_lse = col_max + jnp.log(col_sum + (1.0 - col_live.astype(jnp.float32)))
        row_f = row_live.astype(jnp.float32)
        col_term = jnp.sum(col_live.astype(jnp.float32) * col_lse)
    total = jnp.sum(row_f * (row_lse - 2.0 * pos_score)) + col_term
    pair_loss = (total / live_count.astype(jnp.float32)).reshape(1)

    mine = shard_index * row_count
    a_my = lax.dynamic_slice_in_dim(pair_align, mine, row_count)
    r_my = lax.dynamic_slice_in_dim(row_live, mine, row_count)
    lse_my = lax.dynamic_slice_in_dim(row_lse, mine, row_count)
    pos_rows = perm[None, :] == a_my[:, None]
    s_rows = scores_of(src_emb, y_all, pos_rows, inv_root)
    g_rows = grad_of(s_rows, pos_rows, r_my, col_live, lse_my, col_lse, weight)
    grad_src = (
        jnp.dot(g_rows, y_all, preferred_element_type=jnp.float32) * inv_root
    ).astype(jnp.bfloat16)

    p_my = lax.dynamic_slice_in_dim(perm, mine, row_count)
    c_my = lax.dynamic_slice_in_dim(col_live, mine, row_count)
    clse_my = lax.dynamic_slice_in_dim(col_lse, mine, row_count)
    pos_cols = p_my[None, :] == pair_align[:, None]
    s_cols = scores_of(x_all, partner, pos_cols, inv_root)
    g_cols = grad_of(s_cols, pos_cols, row_live, c_my, row_lse, clse_my, weight)
    own_terms = lax.dot_general(
        g_cols, x_all, (((0,), (0,)), ((), ())), preferred_element_type=jnp.float32
    )
    grad_local = (own_terms * inv_root).astype(jnp.bfloat16)
    returned = lax.all_to_all(
        grad_local.reshape(lang_size, per_slot, emb_width), "lang", split_axis=0, concat_axis=0, tiled=True
    )
    grad_tgt = returned[slot_group]
    return (grad_src, grad_tgt, pair_loss)


def solution(mesh):
    in_specs = (
        P(("lang", "dp"), None),
        P(None, ("lang", "dp"), None),
        P(),
        P(),
        P("lang", None),
        P(),
    )
    out_specs = (P(("lang", "dp"), None), P(None, ("lang", "dp"), None), P("lang"))
    return jax.shard_map(
        functools.partial(per_device, snake_ring(mesh)), mesh=mesh, in_specs=in_specs, out_specs=out_specs, check_vma=False
    )
```

```python
import functools
import math

import jax
import jax.numpy as jnp
from jax import lax
from jax.sharding import PartitionSpec as P

MARGIN = 0.3
LOW_FILL = -1e30
BLOCK_BYTES = 8 * 1024 * 1024


def target_index(col_count, row_count, per_slot, data_size):
    position = jnp.arange(col_count, dtype=jnp.int32)
    source = position // row_count
    within = position % row_count
    return (within // per_slot * data_size + source) * per_slot + within % per_slot


def snake_ring(mesh):
    count = mesh.shape["dp"]
    try:
        spots = [tuple(dev.coords) for dev in mesh.devices.reshape(-1, count)[0]]
    except (AttributeError, TypeError):
        return list(range(count))
    ys = sorted({s[1] for s in spots})
    zs = sorted({s[2] for s in spots})
    where = {(s[1], s[2]): d for d, s in enumerate(spots)}
    if len(where) != count or len(ys) * len(zs) != count:
        return list(range(count))
    rows, cols = (ys, zs) if len(ys) % 2 == 0 else (zs, ys)
    at = lambda r, c: where[(r, c) if rows is ys else (c, r)]
    if len(rows) == 1 or len(cols) == 1:
        return [at(r, c) for r in rows for c in cols]
    order = [at(rows[0], cols[0])]
    for k, r in enumerate(rows):
        seq = cols[1:] if k % 2 == 0 else cols[:0:-1]
        order += [at(r, c) for c in seq]
    order += [at(r, cols[0]) for r in rows[:0:-1]]
    return order


def ring_gather(block, ring, lang_size):
    count = len(ring)
    place = [0] * count
    for p, d in enumerate(ring):
        place[d] = p
    ring_arr = jnp.array(ring, jnp.int32)
    my_dp = lax.axis_index("dp")
    my_pos = jnp.array(place, jnp.int32)[my_dp]
    mirror = 1 - 2 * (lax.axis_index("lang") % 2)

    def pairs_for(even_step):
        out = []
        for l in range(lang_size):
            step = even_step if l % 2 == 0 else -even_step
            out += [(l * count + ring[p], l * count + ring[(p + step) % count]) for p in range(count)]
        return out

    rows = block.shape[0]
    out = jnp.zeros((count * rows,) + block.shape[1:], block.dtype)
    out = lax.dynamic_update_slice_in_dim(out, block, my_dp * rows, 0)
    for even_step, steps in ((1, count // 2), (-1, count - 1 - count // 2)):
        pairs = pairs_for(even_step)
        cur = block
        for t in range(1, steps + 1):
            cur = lax.ppermute(cur, ("lang", "dp"), pairs)
            origin = ring_arr[(my_pos - even_step * mirror * t) % count]
            out = lax.dynamic_update_slice_in_dim(out, cur, origin * rows, 0)
    return out


def sum_free_pick(stack, group):
    rows = stack[0]
    for g in range(1, stack.shape[0]):
        rows = jnp.where(group == g, stack[g], rows)
    return rows


def scores_of(x_rows, y_rows, pos_mask, inv_root):
    raw_dot = lax.dot_general(
        x_rows, y_rows, (((1,), (1,)), ((), ())), preferred_element_type=jnp.float32
    )
    return raw_dot * inv_root - MARGIN * pos_mask.astype(jnp.float32)


def block_stats(scores_f, is_pos, row_live, col_ok):
    row_max = jnp.max(jnp.where(col_ok[None, :], scores_f, LOW_FILL), axis=1)
    row_sum = jnp.sum(
        jnp.where(col_ok[None, :], jnp.exp(scores_f - row_max[:, None]), 0.0), axis=1
    )
    row_lse = row_max + jnp.log(row_sum + (1.0 - row_live.astype(jnp.float32)))
    pos_score = jnp.sum(jnp.where(is_pos, scores_f, 0.0), axis=1)
    col_max = jnp.max(jnp.where(row_live[:, None], scores_f, LOW_FILL), axis=0)
    col_sum = jnp.sum(
        jnp.where(row_live[:, None], jnp.exp(scores_f - col_max[None, :]), 0.0), axis=0
    )
    return row_lse, pos_score, col_max, col_sum


def grad_of(scores_f, is_pos, row_ok, col_ok, row_lse, col_lse, weight):
    both_live = row_ok[:, None] & col_ok[None, :]
    by_row = jnp.where(both_live, jnp.exp(scores_f - row_lse[:, None]), 0.0)
    by_col = jnp.where(both_live, jnp.exp(scores_f - col_lse[None, :]), 0.0)
    pos_hit = (is_pos & row_ok[:, None]).astype(jnp.float32)
    return (weight * (by_row + by_col - 2.0 * pos_hit)).astype(jnp.bfloat16)


def per_device(ring, src_emb, tgt_emb, slot_group, counts, align, pair_weight):
    lang_size = lax.axis_size("lang")
    data_size = lax.axis_size("dp")
    row_count, emb_width = src_emb.shape
    per_slot = tgt_emb.shape[1]
    pair_rows = row_count * data_size
    inv_root = 1.0 / math.sqrt(emb_width)
    group_index = lax.axis_index("lang")
    shard_index = lax.axis_index("dp")
    slot_ids = jnp.arange(lang_size, dtype=jnp.int32)
    slot_of_group = jnp.zeros((lang_size,), jnp.int32).at[slot_group].set(slot_ids)
    ordered = tgt_emb[slot_of_group]
    arrived = lax.all_to_all(ordered, "lang", split_axis=0, concat_axis=1, tiled=True)
    partner = arrived[0]
    live_count = counts[group_index]
    weight = pair_weight[group_index]
    pair_align = align[0]
    all_rows = jnp.arange(pair_rows, dtype=jnp.int32)
    row_live = all_rows < live_count
    perm = target_index(pair_rows, row_count, per_slot, data_size)
    live_pos = (perm[None, :] == pair_align[:, None]) & row_live[:, None]
    col_live = jnp.max(live_pos.astype(jnp.int32), axis=0) > 0
    x_all = ring_gather(src_emb, ring, lang_size)
    y_all = ring_gather(partner, ring, lang_size)

    block = max(1, min(pair_rows, BLOCK_BYTES // (4 * pair_rows)))
    steps = pair_rows // block
    if steps == 1:
        is_pos = perm[None, :] == pair_align[:, None]
        scores_f = scores_of(x_all, y_all, is_pos, inv_root)
        row_lse, pos_score, col_max, col_sum = block_stats(scores_f, is_pos, row_live, col_live)
    else:
        def one_block(k, carry):
            row_lse, pos_score, col_max, col_sum = carry
            start = k * block
            x_blk = lax.dynamic_slice_in_dim(x_all, start, block)
            a_blk = lax.dynamic_slice_in_dim(pair_align, start, block)
            r_blk = lax.dynamic_slice_in_dim(row_live, start, block)
            is_pos = perm[None, :] == a_blk[:, None]
            s_blk = scores_of(x_blk, y_all, is_pos, inv_root)
            b_lse, b_pos, b_max, b_sum = block_stats(s_blk, is_pos, r_blk, col_live)
            top = jnp.maximum(col_max, b_max)
            col_sum = col_sum * jnp.exp(col_max - top) + b_sum * jnp.exp(b_max - top)
            row_lse = lax.dynamic_update_slice_in_dim(row_lse, b_lse, start, 0)
            pos_score = lax.dynamic_update_slice_in_dim(pos_score, b_pos, start, 0)
            return row_lse, pos_score, top, col_sum

        zeros = jnp.zeros((pair_rows,), jnp.float32)
        init = (zeros, zeros, jnp.full((pair_rows,), LOW_FILL, jnp.float32), zeros)
        row_lse, pos_score, col_max, col_sum = lax.fori_loop(0, steps, one_block, init)
    col_lse = col_max + jnp.log(col_sum + (1.0 - col_live.astype(jnp.float32)))

    row_f = row_live.astype(jnp.float32)
    col_f = col_live.astype(jnp.float32)
    total = jnp.sum(row_f * (row_lse - 2.0 * pos_score)) + jnp.sum(col_f * col_lse)
    pair_loss = (total / live_count.astype(jnp.float32)).reshape(1)

    mine = shard_index * row_count
    a_my = lax.dynamic_slice_in_dim(pair_align, mine, row_count)
    r_my = lax.dynamic_slice_in_dim(row_live, mine, row_count)
    lse_my = lax.dynamic_slice_in_dim(row_lse, mine, row_count)
    pos_rows = perm[None, :] == a_my[:, None]
    s_rows = scores_of(src_emb, y_all, pos_rows, inv_root)
    g_rows = grad_of(s_rows, pos_rows, r_my, col_live, lse_my, col_lse, weight)
    grad_src = (
        jnp.dot(g_rows, y_all, preferred_element_type=jnp.float32) * inv_root
    ).astype(jnp.bfloat16)

    p_my = lax.dynamic_slice_in_dim(perm, mine, row_count)
    c_my = lax.dynamic_slice_in_dim(col_live, mine, row_count)
    clse_my = lax.dynamic_slice_in_dim(col_lse, mine, row_count)
    pos_cols = p_my[None, :] == pair_align[:, None]
    s_cols = scores_of(x_all, partner, pos_cols, inv_root)
    g_cols = grad_of(s_cols, pos_cols, row_live, c_my, row_lse, clse_my, weight)
    own_terms = lax.dot_general(
        g_cols, x_all, (((0,), (0,)), ((), ())), preferred_element_type=jnp.float32
    )
    grad_local = (own_terms * inv_root).astype(jnp.bfloat16)
    returned = lax.all_to_all(
        grad_local.reshape(lang_size, per_slot, emb_width), "lang", split_axis=0, concat_axis=0, tiled=True
    )
    grad_tgt = jnp.stack(
        [
            sum_free_pick(returned, slot_group[slot])
            for slot in range(lang_size)
        ]
    )
    return (grad_src, grad_tgt, pair_loss)


def solution(mesh):
    in_specs = (
        P(("lang", "dp"), None),
        P(None, ("lang", "dp"), None),
        P(),
        P(),
        P("lang", None),
        P(),
    )
    out_specs = (P(("lang", "dp"), None), P(None, ("lang", "dp"), None), P("lang"))
    return jax.shard_map(
        functools.partial(per_device, snake_ring(mesh)), mesh=mesh, in_specs=in_specs, out_specs=out_specs, check_vma=False
    )
```

```python
import functools
import math

import jax
import jax.numpy as jnp
from jax import lax
from jax.sharding import PartitionSpec as P

MARGIN = 0.3
LOW_FILL = -1e30
BLOCK_BYTES = 8 * 1024 * 1024


def target_index(col_count, row_count, per_slot, data_size):
    position = jnp.arange(col_count, dtype=jnp.int32)
    source = position // row_count
    within = position % row_count
    return (within // per_slot * data_size + source) * per_slot + within % per_slot


def snake_ring(mesh):
    count = mesh.shape["dp"]
    try:
        spots = [tuple(dev.coords) for dev in mesh.devices.reshape(-1, count)[0]]
    except (AttributeError, TypeError):
        return list(range(count))
    ys = sorted({s[1] for s in spots})
    zs = sorted({s[2] for s in spots})
    where = {(s[1], s[2]): d for d, s in enumerate(spots)}
    if len(where) != count or len(ys) * len(zs) != count:
        return list(range(count))
    rows, cols = (ys, zs) if len(ys) % 2 == 0 else (zs, ys)
    at = lambda r, c: where[(r, c) if rows is ys else (c, r)]
    if len(rows) == 1 or len(cols) == 1:
        return [at(r, c) for r in rows for c in cols]
    order = [at(rows[0], cols[0])]
    for k, r in enumerate(rows):
        seq = cols[1:] if k % 2 == 0 else cols[:0:-1]
        order += [at(r, c) for c in seq]
    order += [at(r, cols[0]) for r in rows[:0:-1]]
    return order


def ring_gather(block, ring, lang_size):
    count = len(ring)
    place = [0] * count
    for p, d in enumerate(ring):
        place[d] = p
    ring_arr = jnp.array(ring, jnp.int32)
    my_dp = lax.axis_index("dp")
    my_pos = jnp.array(place, jnp.int32)[my_dp]
    mirror = 1 - 2 * (lax.axis_index("lang") % 2)

    def pairs_for(even_step):
        out = []
        for l in range(lang_size):
            step = even_step if l % 2 == 0 else -even_step
            out += [(l * count + ring[p], l * count + ring[(p + step) % count]) for p in range(count)]
        return out

    rows = block.shape[0]
    out = jnp.zeros((count * rows,) + block.shape[1:], block.dtype)
    out = lax.dynamic_update_slice_in_dim(out, block, my_dp * rows, 0)
    for even_step, steps in ((1, count // 2), (-1, count - 1 - count // 2)):
        pairs = pairs_for(even_step)
        cur = block
        for t in range(1, steps + 1):
            cur = lax.ppermute(cur, ("lang", "dp"), pairs)
            origin = ring_arr[(my_pos - even_step * mirror * t) % count]
            out = lax.dynamic_update_slice_in_dim(out, cur, origin * rows, 0)
    return out


def scores_of(x_rows, y_rows, pos_mask, inv_root):
    raw_dot = lax.dot_general(
        x_rows, y_rows, (((1,), (1,)), ((), ())), preferred_element_type=jnp.float32
    )
    return raw_dot * inv_root - MARGIN * pos_mask.astype(jnp.float32)


def block_stats(scores_f, is_pos, row_live, col_ok):
    row_max = jnp.max(jnp.where(col_ok[None, :], scores_f, LOW_FILL), axis=1)
    row_sum = jnp.sum(
        jnp.where(col_ok[None, :], jnp.exp(scores_f - row_max[:, None]), 0.0), axis=1
    )
    row_lse = row_max + jnp.log(row_sum + (1.0 - row_live.astype(jnp.float32)))
    pos_score = jnp.sum(jnp.where(is_pos, scores_f, 0.0), axis=1)
    col_max = jnp.max(jnp.where(row_live[:, None], scores_f, LOW_FILL), axis=0)
    col_sum = jnp.sum(
        jnp.where(row_live[:, None], jnp.exp(scores_f - col_max[None, :]), 0.0), axis=0
    )
    return row_lse, pos_score, col_max, col_sum


def grad_of(scores_f, is_pos, row_ok, col_ok, row_lse, col_lse, weight):
    both_live = row_ok[:, None] & col_ok[None, :]
    by_row = jnp.where(both_live, jnp.exp(scores_f - row_lse[:, None]), 0.0)
    by_col = jnp.where(both_live, jnp.exp(scores_f - col_lse[None, :]), 0.0)
    pos_hit = (is_pos & row_ok[:, None]).astype(jnp.float32)
    return (weight * (by_row + by_col - 2.0 * pos_hit)).astype(jnp.bfloat16)


def per_device(ring, src_emb, tgt_emb, slot_group, counts, align, pair_weight):
    lang_size = lax.axis_size("lang")
    data_size = lax.axis_size("dp")
    row_count, emb_width = src_emb.shape
    per_slot = tgt_emb.shape[1]
    pair_rows = row_count * data_size
    inv_root = 1.0 / math.sqrt(emb_width)
    group_index = lax.axis_index("lang")
    shard_index = lax.axis_index("dp")
    slot_ids = jnp.arange(lang_size, dtype=jnp.int32)
    slot_of_group = jnp.zeros((lang_size,), jnp.int32).at[slot_group].set(slot_ids)
    ordered = tgt_emb[slot_of_group]
    arrived = lax.all_to_all(ordered, "lang", split_axis=0, concat_axis=1, tiled=True)
    partner = arrived[0]
    live_count = counts[group_index]
    weight = pair_weight[group_index]
    pair_align = align[0]
    all_rows = jnp.arange(pair_rows, dtype=jnp.int32)
    row_live = all_rows < live_count
    perm = target_index(pair_rows, row_count, per_slot, data_size)
    live_pos = (perm[None, :] == pair_align[:, None]) & row_live[:, None]
    col_live = jnp.max(live_pos.astype(jnp.int32), axis=0) > 0
    x_all = ring_gather(src_emb, ring, lang_size)
    y_all = ring_gather(partner, ring, lang_size)

    block = max(1, min(pair_rows, BLOCK_BYTES // (4 * pair_rows)))
    steps = pair_rows // block
    if steps == 1:
        is_pos = perm[None, :] == pair_align[:, None]
        scores_f = scores_of(x_all, y_all, is_pos, inv_root)
        row_lse, pos_score, col_max, col_sum = block_stats(scores_f, is_pos, row_live, col_live)
    else:
        def one_block(k, carry):
            row_lse, pos_score, col_max, col_sum = carry
            start = k * block
            x_blk = lax.dynamic_slice_in_dim(x_all, start, block)
            a_blk = lax.dynamic_slice_in_dim(pair_align, start, block)
            r_blk = lax.dynamic_slice_in_dim(row_live, start, block)
            is_pos = perm[None, :] == a_blk[:, None]
            s_blk = scores_of(x_blk, y_all, is_pos, inv_root)
            b_lse, b_pos, b_max, b_sum = block_stats(s_blk, is_pos, r_blk, col_live)
            top = jnp.maximum(col_max, b_max)
            col_sum = col_sum * jnp.exp(col_max - top) + b_sum * jnp.exp(b_max - top)
            row_lse = lax.dynamic_update_slice_in_dim(row_lse, b_lse, start, 0)
            pos_score = lax.dynamic_update_slice_in_dim(pos_score, b_pos, start, 0)
            return row_lse, pos_score, top, col_sum

        zeros = jnp.zeros((pair_rows,), jnp.float32)
        init = (zeros, zeros, jnp.full((pair_rows,), LOW_FILL, jnp.float32), zeros)
        row_lse, pos_score, col_max, col_sum = lax.fori_loop(0, steps, one_block, init)
    col_lse = col_max + jnp.log(col_sum + (1.0 - col_live.astype(jnp.float32)))

    row_f = row_live.astype(jnp.float32)
    col_f = col_live.astype(jnp.float32)
    total = jnp.sum(row_f * (row_lse - 2.0 * pos_score)) + jnp.sum(col_f * col_lse)

    mine = shard_index * row_count
    a_my = lax.dynamic_slice_in_dim(pair_align, mine, row_count)
    r_my = lax.dynamic_slice_in_dim(row_live, mine, row_count)
    lse_my = lax.dynamic_slice_in_dim(row_lse, mine, row_count)
    pos_rows = perm[None, :] == a_my[:, None]
    s_rows = scores_of(src_emb, y_all, pos_rows, inv_root)
    g_rows = grad_of(s_rows, pos_rows, r_my, col_live, lse_my, col_lse, weight)
    grad_src = (
        jnp.dot(g_rows, y_all, preferred_element_type=jnp.float32) * inv_root
    ).astype(jnp.bfloat16)

    p_my = lax.dynamic_slice_in_dim(perm, mine, row_count)
    c_my = lax.dynamic_slice_in_dim(col_live, mine, row_count)
    clse_my = lax.dynamic_slice_in_dim(col_lse, mine, row_count)
    pos_cols = p_my[None, :] == pair_align[:, None]
    s_cols = scores_of(x_all, partner, pos_cols, inv_root)
    g_cols = grad_of(s_cols, pos_cols, row_live, c_my, row_lse, clse_my, weight)
    own_terms = lax.dot_general(
        g_cols, x_all, (((0,), (0,)), ((), ())), preferred_element_type=jnp.float32
    )
    grad_local = (own_terms * inv_root).astype(jnp.bfloat16)
    total = total + 0.0 * grad_local[0, 0].astype(jnp.float32)
    pair_loss = (total / live_count.astype(jnp.float32)).reshape(1)
    returned = lax.all_to_all(
        grad_local.reshape(lang_size, per_slot, emb_width), "lang", split_axis=0, concat_axis=0, tiled=True
    )
    grad_tgt = returned[slot_group]
    return (grad_src, grad_tgt, pair_loss)


def solution(mesh):
    in_specs = (
        P(("lang", "dp"), None),
        P(None, ("lang", "dp"), None),
        P(),
        P(),
        P("lang", None),
        P(),
    )
    out_specs = (P(("lang", "dp"), None), P(None, ("lang", "dp"), None), P("lang"))
    return jax.shard_map(
        functools.partial(per_device, snake_ring(mesh)), mesh=mesh, in_specs=in_specs, out_specs=out_specs, check_vma=False
    )
```

```python
import functools
import math

import jax
import jax.numpy as jnp
from jax import lax
from jax.sharding import PartitionSpec as P

MARGIN = 0.3
LOW_FILL = -1e30
BLOCK_BYTES = 8 * 1024 * 1024


def target_index(col_count, row_count, per_slot, data_size):
    position = jnp.arange(col_count, dtype=jnp.int32)
    source = position // row_count
    within = position % row_count
    return (within // per_slot * data_size + source) * per_slot + within % per_slot


def snake_ring(mesh):
    count = mesh.shape["dp"]
    try:
        spots = [tuple(dev.coords) for dev in mesh.devices.reshape(-1, count)[0]]
    except (AttributeError, TypeError):
        return list(range(count))
    ys = sorted({s[1] for s in spots})
    zs = sorted({s[2] for s in spots})
    where = {(s[1], s[2]): d for d, s in enumerate(spots)}
    if len(where) != count or len(ys) * len(zs) != count:
        return list(range(count))
    rows, cols = (ys, zs) if len(ys) % 2 == 0 else (zs, ys)
    at = lambda r, c: where[(r, c) if rows is ys else (c, r)]
    if len(rows) == 1 or len(cols) == 1:
        return [at(r, c) for r in rows for c in cols]
    order = [at(rows[0], cols[0])]
    for k, r in enumerate(rows):
        seq = cols[1:] if k % 2 == 0 else cols[:0:-1]
        order += [at(r, c) for c in seq]
    order += [at(r, cols[0]) for r in rows[:0:-1]]
    return order


def ring_gather(block, ring, lang_size):
    count = len(ring)
    place = [0] * count
    for p, d in enumerate(ring):
        place[d] = p
    ring_arr = jnp.array(ring, jnp.int32)
    my_dp = lax.axis_index("dp")
    my_pos = jnp.array(place, jnp.int32)[my_dp]
    mirror = 1 - 2 * (lax.axis_index("lang") % 2)

    def pairs_for(even_step):
        out = []
        for l in range(lang_size):
            step = even_step if l % 2 == 0 else -even_step
            out += [(l * count + ring[p], l * count + ring[(p + step) % count]) for p in range(count)]
        return out

    rows = block.shape[0]
    out = jnp.zeros((count * rows,) + block.shape[1:], block.dtype)
    out = lax.dynamic_update_slice_in_dim(out, block, my_dp * rows, 0)
    for even_step, steps in ((1, count // 2), (-1, count - 1 - count // 2)):
        pairs = pairs_for(even_step)
        cur = block
        for t in range(1, steps + 1):
            cur = lax.ppermute(cur, ("lang", "dp"), pairs)
            origin = ring_arr[(my_pos - even_step * mirror * t) % count]
            out = lax.dynamic_update_slice_in_dim(out, cur, origin * rows, 0)
    return out


def scores_of(x_rows, y_rows, pos_mask, inv_root):
    raw_dot = lax.dot_general(
        x_rows, y_rows, (((1,), (1,)), ((), ())), preferred_element_type=jnp.float32
    )
    return raw_dot * inv_root - MARGIN * pos_mask.astype(jnp.float32)


def block_stats(scores_f, is_pos, row_live, col_ok):
    row_max = jnp.max(jnp.where(col_ok[None, :], scores_f, LOW_FILL), axis=1)
    row_sum = jnp.sum(
        jnp.where(col_ok[None, :], jnp.exp(scores_f - row_max[:, None]), 0.0), axis=1
    )
    row_lse = row_max + jnp.log(row_sum + (1.0 - row_live.astype(jnp.float32)))
    pos_score = jnp.sum(jnp.where(is_pos, scores_f, 0.0), axis=1)
    col_max = jnp.max(jnp.where(row_live[:, None], scores_f, LOW_FILL), axis=0)
    col_sum = jnp.sum(
        jnp.where(row_live[:, None], jnp.exp(scores_f - col_max[None, :]), 0.0), axis=0
    )
    return row_lse, pos_score, col_max, col_sum


def grad_of(scores_f, is_pos, row_ok, col_ok, row_lse, col_lse, weight):
    both_live = row_ok[:, None] & col_ok[None, :]
    by_row = jnp.where(both_live, jnp.exp(scores_f - row_lse[:, None]), 0.0)
    by_col = jnp.where(both_live, jnp.exp(scores_f - col_lse[None, :]), 0.0)
    pos_hit = (is_pos & row_ok[:, None]).astype(jnp.float32)
    return (weight * (by_row + by_col - 2.0 * pos_hit)).astype(jnp.bfloat16)


def per_device(ring, src_emb, tgt_emb, slot_group, counts, align, pair_weight):
    lang_size = lax.axis_size("lang")
    data_size = lax.axis_size("dp")
    row_count, emb_width = src_emb.shape
    per_slot = tgt_emb.shape[1]
    pair_rows = row_count * data_size
    inv_root = 1.0 / math.sqrt(emb_width)
    group_index = lax.axis_index("lang")
    shard_index = lax.axis_index("dp")
    slot_ids = jnp.arange(lang_size, dtype=jnp.int32)
    slot_of_group = jnp.zeros((lang_size,), jnp.int32).at[slot_group].set(slot_ids)
    ordered = tgt_emb[slot_of_group]
    arrived = lax.all_to_all(ordered, "lang", split_axis=0, concat_axis=1, tiled=True)
    partner = arrived[0]
    live_count = counts[group_index]
    weight = pair_weight[group_index]
    pair_align = align[0]
    all_rows = jnp.arange(pair_rows, dtype=jnp.int32)
    row_live = all_rows < live_count
    perm = target_index(pair_rows, row_count, per_slot, data_size)
    live_pos = (perm[None, :] == pair_align[:, None]) & row_live[:, None]
    col_live = jnp.max(live_pos.astype(jnp.int32), axis=0) > 0
    x_all = ring_gather(src_emb, ring, lang_size)
    y_all = ring_gather(partner, ring, lang_size)

    block = max(1, min(pair_rows, BLOCK_BYTES // (4 * pair_rows)))
    steps = pair_rows // block
    if steps == 1:
        is_pos = perm[None, :] == pair_align[:, None]
        scores_f = scores_of(x_all, y_all, is_pos, inv_root)
        row_lse, pos_score, col_max, col_sum = block_stats(scores_f, is_pos, row_live, col_live)
    else:
        def one_block(k, carry):
            row_lse, pos_score, col_max, col_sum = carry
            start = k * block
            x_blk = lax.dynamic_slice_in_dim(x_all, start, block)
            a_blk = lax.dynamic_slice_in_dim(pair_align, start, block)
            r_blk = lax.dynamic_slice_in_dim(row_live, start, block)
            is_pos = perm[None, :] == a_blk[:, None]
            s_blk = scores_of(x_blk, y_all, is_pos, inv_root)
            b_lse, b_pos, b_max, b_sum = block_stats(s_blk, is_pos, r_blk, col_live)
            top = jnp.maximum(col_max, b_max)
            col_sum = col_sum * jnp.exp(col_max - top) + b_sum * jnp.exp(b_max - top)
            row_lse = lax.dynamic_update_slice_in_dim(row_lse, b_lse, start, 0)
            pos_score = lax.dynamic_update_slice_in_dim(pos_score, b_pos, start, 0)
            return row_lse, pos_score, top, col_sum

        zeros = jnp.zeros((pair_rows,), jnp.float32)
        init = (zeros, zeros, jnp.full((pair_rows,), LOW_FILL, jnp.float32), zeros)
        row_lse, pos_score, col_max, col_sum = lax.fori_loop(0, steps, one_block, init)
    col_lse = col_max + jnp.log(col_sum + (1.0 - col_live.astype(jnp.float32)))

    row_f = row_live.astype(jnp.float32)
    col_f = col_live.astype(jnp.float32)
    total = jnp.sum(row_f * (row_lse - 2.0 * pos_score)) + jnp.sum(col_f * col_lse)
    pair_loss = (total / live_count.astype(jnp.float32)).reshape(1)

    mine = shard_index * row_count
    a_my = lax.dynamic_slice_in_dim(pair_align, mine, row_count)
    r_my = (mine + jnp.arange(row_count, dtype=jnp.int32)) < live_count
    lse_my = lax.dynamic_slice_in_dim(row_lse, mine, row_count)
    pos_rows = perm[None, :] == a_my[:, None]
    s_rows = scores_of(src_emb, y_all, pos_rows, inv_root)
    g_rows = grad_of(s_rows, pos_rows, r_my, col_live, lse_my, col_lse, weight)
    grad_src = (
        jnp.dot(g_rows, y_all, preferred_element_type=jnp.float32) * inv_root
    ).astype(jnp.bfloat16)

    q_my = jnp.arange(row_count, dtype=jnp.int32)
    p_my = (q_my // per_slot * data_size + shard_index) * per_slot + q_my % per_slot
    clse_my = lax.dynamic_slice_in_dim(col_lse, mine, row_count)
    pos_cols = p_my[None, :] == pair_align[:, None]
    c_my = jnp.max((pos_cols & row_live[:, None]).astype(jnp.int32), axis=0) > 0
    s_cols = scores_of(x_all, partner, pos_cols, inv_root)
    g_cols = grad_of(s_cols, pos_cols, row_live, c_my, row_lse, clse_my, weight)
    own_terms = lax.dot_general(
        g_cols, x_all, (((0,), (0,)), ((), ())), preferred_element_type=jnp.float32
    )
    grad_local = (own_terms * inv_root).astype(jnp.bfloat16)
    returned = lax.all_to_all(
        grad_local.reshape(lang_size, per_slot, emb_width), "lang", split_axis=0, concat_axis=0, tiled=True
    )
    grad_tgt = returned[slot_group]
    return (grad_src, grad_tgt, pair_loss)


def solution(mesh):
    in_specs = (
        P(("lang", "dp"), None),
        P(None, ("lang", "dp"), None),
        P(),
        P(),
        P("lang", None),
        P(),
    )
    out_specs = (P(("lang", "dp"), None), P(None, ("lang", "dp"), None), P("lang"))
    return jax.shard_map(
        functools.partial(per_device, snake_ring(mesh)), mesh=mesh, in_specs=in_specs, out_specs=out_specs, check_vma=False
    )
```

```python
import functools
import math

import jax
import jax.numpy as jnp
from jax import lax
from jax.sharding import PartitionSpec as P

MARGIN = 0.3
LOW_FILL = -1e30
BLOCK_BYTES = 8 * 1024 * 1024


def target_index(col_count, row_count, per_slot, data_size):
    position = jnp.arange(col_count, dtype=jnp.int32)
    source = position // row_count
    within = position % row_count
    return (within // per_slot * data_size + source) * per_slot + within % per_slot


def snake_ring(mesh):
    count = mesh.shape["dp"]
    try:
        spots = [tuple(dev.coords) for dev in mesh.devices.reshape(-1, count)[0]]
    except (AttributeError, TypeError):
        return list(range(count))
    ys = sorted({s[1] for s in spots})
    zs = sorted({s[2] for s in spots})
    where = {(s[1], s[2]): d for d, s in enumerate(spots)}
    if len(where) != count or len(ys) * len(zs) != count:
        return list(range(count))
    rows, cols = (ys, zs) if len(ys) % 2 == 0 else (zs, ys)
    at = lambda r, c: where[(r, c) if rows is ys else (c, r)]
    if len(rows) == 1 or len(cols) == 1:
        return [at(r, c) for r in rows for c in cols]
    order = [at(rows[0], cols[0])]
    for k, r in enumerate(rows):
        seq = cols[1:] if k % 2 == 0 else cols[:0:-1]
        order += [at(r, c) for c in seq]
    order += [at(r, cols[0]) for r in rows[:0:-1]]
    return order


def ring_gather(block, ring, lang_size):
    count = len(ring)
    place = [0] * count
    for p, d in enumerate(ring):
        place[d] = p
    ring_arr = jnp.array(ring, jnp.int32)
    my_dp = lax.axis_index("dp")
    my_pos = jnp.array(place, jnp.int32)[my_dp]
    mirror = 1 - 2 * (lax.axis_index("lang") % 2)

    def pairs_for(even_step):
        out = []
        for l in range(lang_size):
            step = even_step if l % 2 == 0 else -even_step
            out += [(l * count + ring[p], l * count + ring[(p + step) % count]) for p in range(count)]
        return out

    rows = block.shape[0]
    out = jnp.zeros((count * rows,) + block.shape[1:], block.dtype)
    out = lax.dynamic_update_slice_in_dim(out, block, my_dp * rows, 0)
    for even_step, steps in ((1, count // 2), (-1, count - 1 - count // 2)):
        pairs = pairs_for(even_step)
        cur = block
        for t in range(1, steps + 1):
            cur = lax.ppermute(cur, ("lang", "dp"), pairs)
            origin = ring_arr[(my_pos - even_step * mirror * t) % count]
            out = lax.dynamic_update_slice_in_dim(out, cur, origin * rows, 0)
    return out


def scores_of(x_rows, y_rows, pos_mask, inv_root):
    raw_dot = lax.dot_general(
        x_rows, y_rows, (((1,), (1,)), ((), ())), preferred_element_type=jnp.float32
    )
    return raw_dot * inv_root - MARGIN * pos_mask.astype(jnp.float32)


def block_stats(scores_f, is_pos, row_live, col_ok):
    row_max = jnp.max(jnp.where(col_ok[None, :], scores_f, LOW_FILL), axis=1)
    row_sum = jnp.sum(
        jnp.where(col_ok[None, :], jnp.exp(scores_f - row_max[:, None]), 0.0), axis=1
    )
    row_lse = row_max + jnp.log(row_sum + (1.0 - row_live.astype(jnp.float32)))
    pos_score = jnp.sum(jnp.where(is_pos, scores_f, 0.0), axis=1)
    col_max = jnp.max(jnp.where(row_live[:, None], scores_f, LOW_FILL), axis=0)
    col_sum = jnp.sum(
        jnp.where(row_live[:, None], jnp.exp(scores_f - col_max[None, :]), 0.0), axis=0
    )
    return row_lse, pos_score, col_max, col_sum


def grad_of(scores_f, is_pos, row_ok, col_ok, row_lse, col_lse, weight):
    both_live = row_ok[:, None] & col_ok[None, :]
    by_row = jnp.where(both_live, jnp.exp(scores_f - row_lse[:, None]), 0.0)
    by_col = jnp.where(both_live, jnp.exp(scores_f - col_lse[None, :]), 0.0)
    pos_hit = (is_pos & row_ok[:, None]).astype(jnp.float32)
    return (weight * (by_row + by_col - 2.0 * pos_hit)).astype(jnp.bfloat16)


def per_device(ring, src_emb, tgt_emb, slot_group, counts, align, pair_weight):
    lang_size = lax.axis_size("lang")
    data_size = lax.axis_size("dp")
    row_count, emb_width = src_emb.shape
    per_slot = tgt_emb.shape[1]
    pair_rows = row_count * data_size
    inv_root = 1.0 / math.sqrt(emb_width)
    group_index = lax.axis_index("lang")
    shard_index = lax.axis_index("dp")
    slot_ids = jnp.arange(lang_size, dtype=jnp.int32)
    slot_of_group = jnp.zeros((lang_size,), jnp.int32).at[slot_group].set(slot_ids)
    ordered = tgt_emb[slot_of_group]
    arrived = lax.all_to_all(ordered, "lang", split_axis=0, concat_axis=1, tiled=True)
    partner = arrived[0]
    live_count = counts[group_index]
    weight = pair_weight[group_index]
    pair_align = align[0]
    all_rows = jnp.arange(pair_rows, dtype=jnp.int32)
    row_live = all_rows < live_count
    perm = target_index(pair_rows, row_count, per_slot, data_size)
    live_pos = (perm[None, :] == pair_align[:, None]) & row_live[:, None]
    col_live = jnp.max(live_pos.astype(jnp.int32), axis=0) > 0
    x_all = ring_gather(src_emb, ring, lang_size)
    y_all = ring_gather(partner, ring, lang_size)

    block = max(1, min(pair_rows, BLOCK_BYTES // (4 * pair_rows)))
    steps = pair_rows // block
    if steps == 1:
        is_pos = perm[None, :] == pair_align[:, None]
        scores_f = scores_of(x_all, y_all, is_pos, inv_root)
        row_lse, pos_score, col_max, col_sum = block_stats(scores_f, is_pos, row_live, col_live)
    else:
        def one_block(k, carry):
            row_lse, pos_score, col_max, col_sum = carry
            start = k * block
            x_blk = lax.dynamic_slice_in_dim(x_all, start, block)
            a_blk = lax.dynamic_slice_in_dim(pair_align, start, block)
            r_blk = lax.dynamic_slice_in_dim(row_live, start, block)
            is_pos = perm[None, :] == a_blk[:, None]
            s_blk = scores_of(x_blk, y_all, is_pos, inv_root)
            b_lse, b_pos, b_max, b_sum = block_stats(s_blk, is_pos, r_blk, col_live)
            top = jnp.maximum(col_max, b_max)
            col_sum = col_sum * jnp.exp(col_max - top) + b_sum * jnp.exp(b_max - top)
            row_lse = lax.dynamic_update_slice_in_dim(row_lse, b_lse, start, 0)
            pos_score = lax.dynamic_update_slice_in_dim(pos_score, b_pos, start, 0)
            return row_lse, pos_score, top, col_sum

        zeros = jnp.zeros((pair_rows,), jnp.float32)
        init = (zeros, zeros, jnp.full((pair_rows,), LOW_FILL, jnp.float32), zeros)
        row_lse, pos_score, col_max, col_sum = lax.fori_loop(0, steps, one_block, init)
    col_lse = col_max + jnp.log(col_sum + (1.0 - col_live.astype(jnp.float32)))

    row_f = row_live.astype(jnp.float32)
    col_f = col_live.astype(jnp.float32)
    total = jnp.sum(row_f * (row_lse - 2.0 * pos_score)) + jnp.sum(col_f * col_lse)
    pair_loss = (total / live_count.astype(jnp.float32)).reshape(1)

    mine = shard_index * row_count
    a_my = lax.dynamic_slice_in_dim(pair_align, mine, row_count)
    r_my = (mine + jnp.arange(row_count, dtype=jnp.int32)) < live_count
    lse_my = lax.dynamic_slice_in_dim(row_lse, mine, row_count)
    pos_rows = perm[None, :] == a_my[:, None]
    s_rows = scores_of(src_emb, y_all, pos_rows, inv_root)
    g_rows = grad_of(s_rows, pos_rows, r_my, col_live, lse_my, col_lse, weight)
    grad_src = (
        jnp.dot(g_rows, y_all, preferred_element_type=jnp.float32) * inv_root
    ).astype(jnp.bfloat16)

    q_my = jnp.arange(row_count, dtype=jnp.int32)
    p_my = (q_my // per_slot * data_size + shard_index) * per_slot + q_my % per_slot
    clse_my = lax.dynamic_slice_in_dim(col_lse, mine, row_count)
    pos_cols = p_my[None, :] == pair_align[:, None]
    c_my = jnp.max((pos_cols & row_live[:, None]).astype(jnp.int32), axis=0) > 0
    s_cols = scores_of(x_all, partner, pos_cols, inv_root)
    g_cols = grad_of(s_cols, pos_cols, row_live, c_my, row_lse, clse_my, weight)
    own_terms = lax.dot_general(
        g_cols, x_all, (((0,), (0,)), ((), ())), preferred_element_type=jnp.float32
    )
    grad_local = (own_terms * inv_root).astype(jnp.bfloat16)
    returned = lax.all_to_all(
        grad_local.reshape(lang_size, per_slot, emb_width), "lang", split_axis=0, concat_axis=0, tiled=True
    )
    choose = (slot_group[:, None] == jnp.arange(lang_size, dtype=jnp.int32)[None, :]).astype(returned.dtype)
    grad_tgt = jnp.einsum(
        "sg,grd->srd", choose, returned, preferred_element_type=jnp.float32
    ).astype(returned.dtype)
    return (grad_src, grad_tgt, pair_loss)


def solution(mesh):
    in_specs = (
        P(("lang", "dp"), None),
        P(None, ("lang", "dp"), None),
        P(),
        P(),
        P("lang", None),
        P(),
    )
    out_specs = (P(("lang", "dp"), None), P(None, ("lang", "dp"), None), P("lang"))
    return jax.shard_map(
        functools.partial(per_device, snake_ring(mesh)), mesh=mesh, in_specs=in_specs, out_specs=out_specs, check_vma=False
    )
```

```python
import functools
import math

import jax
import jax.numpy as jnp
from jax import lax
from jax.sharding import PartitionSpec as P

MARGIN = 0.3
LOW_FILL = -1e30
BLOCK_BYTES = 8 * 1024 * 1024


def target_index(col_count, row_count, per_slot, data_size):
    position = jnp.arange(col_count, dtype=jnp.int32)
    source = position // row_count
    within = position % row_count
    return (within // per_slot * data_size + source) * per_slot + within % per_slot


def snake_ring(mesh):
    count = mesh.shape["dp"]
    try:
        spots = [tuple(dev.coords) for dev in mesh.devices.reshape(-1, count)[0]]
    except (AttributeError, TypeError):
        return list(range(count))
    ys = sorted({s[1] for s in spots})
    zs = sorted({s[2] for s in spots})
    where = {(s[1], s[2]): d for d, s in enumerate(spots)}
    if len(where) != count or len(ys) * len(zs) != count:
        return list(range(count))
    rows, cols = (ys, zs) if len(ys) % 2 == 0 else (zs, ys)
    at = lambda r, c: where[(r, c) if rows is ys else (c, r)]
    if len(rows) == 1 or len(cols) == 1:
        return [at(r, c) for r in rows for c in cols]
    order = [at(rows[0], cols[0])]
    for k, r in enumerate(rows):
        seq = cols[1:] if k % 2 == 0 else cols[:0:-1]
        order += [at(r, c) for c in seq]
    order += [at(r, cols[0]) for r in rows[:0:-1]]
    return order


def ring_gather(block, ring, lang_size):
    count = len(ring)
    place = [0] * count
    for p, d in enumerate(ring):
        place[d] = p
    ring_arr = jnp.array(ring, jnp.int32)
    my_dp = lax.axis_index("dp")
    my_pos = jnp.array(place, jnp.int32)[my_dp]
    mirror = 1 - 2 * (lax.axis_index("lang") % 2)

    def pairs_for(even_step):
        out = []
        for l in range(lang_size):
            step = even_step if l % 2 == 0 else -even_step
            out += [(l * count + ring[p], l * count + ring[(p + step) % count]) for p in range(count)]
        return out

    rows = block.shape[0]
    out = jnp.zeros((count * rows,) + block.shape[1:], block.dtype)
    out = lax.dynamic_update_slice_in_dim(out, block, my_dp * rows, 0)
    for even_step, steps in ((1, count // 2), (-1, count - 1 - count // 2)):
        pairs = pairs_for(even_step)
        cur = block
        for t in range(1, steps + 1):
            cur = lax.ppermute(cur, ("lang", "dp"), pairs)
            origin = ring_arr[(my_pos - even_step * mirror * t) % count]
            out = lax.dynamic_update_slice_in_dim(out, cur, origin * rows, 0)
    return out


def scores_of(x_rows, y_rows, pos_mask, inv_root):
    raw_dot = lax.dot_general(
        x_rows, y_rows, (((1,), (1,)), ((), ())), preferred_element_type=jnp.float32
    )
    return raw_dot * inv_root - MARGIN * pos_mask.astype(jnp.float32)


def block_stats(scores_f, is_pos, row_live, col_ok):
    row_max = jnp.max(jnp.where(col_ok[None, :], scores_f, LOW_FILL), axis=1)
    row_sum = jnp.sum(
        jnp.where(col_ok[None, :], jnp.exp(scores_f - row_max[:, None]), 0.0), axis=1
    )
    row_lse = row_max + jnp.log(row_sum + (1.0 - row_live.astype(jnp.float32)))
    pos_score = jnp.sum(jnp.where(is_pos, scores_f, 0.0), axis=1)
    col_max = jnp.max(jnp.where(row_live[:, None], scores_f, LOW_FILL), axis=0)
    col_sum = jnp.sum(
        jnp.where(row_live[:, None], jnp.exp(scores_f - col_max[None, :]), 0.0), axis=0
    )
    return row_lse, pos_score, col_max, col_sum


def grad_of(scores_f, is_pos, row_ok, col_ok, row_lse, col_lse, weight):
    both_live = row_ok[:, None] & col_ok[None, :]
    by_row = jnp.where(both_live, jnp.exp(scores_f - row_lse[:, None]), 0.0)
    by_col = jnp.where(both_live, jnp.exp(scores_f - col_lse[None, :]), 0.0)
    pos_hit = (is_pos & row_ok[:, None]).astype(jnp.float32)
    return (weight * (by_row + by_col - 2.0 * pos_hit)).astype(jnp.bfloat16)


def per_device(ring, src_emb, tgt_emb, slot_group, counts, align, pair_weight):
    lang_size = lax.axis_size("lang")
    data_size = lax.axis_size("dp")
    row_count, emb_width = src_emb.shape
    per_slot = tgt_emb.shape[1]
    pair_rows = row_count * data_size
    inv_root = 1.0 / math.sqrt(emb_width)
    group_index = lax.axis_index("lang")
    shard_index = lax.axis_index("dp")
    slot_ids = jnp.arange(lang_size, dtype=jnp.int32)
    slot_of_group = jnp.zeros((lang_size,), jnp.int32).at[slot_group].set(slot_ids)
    ordered = tgt_emb[slot_of_group]
    arrived = lax.all_to_all(ordered, "lang", split_axis=0, concat_axis=1, tiled=True)
    partner = arrived[0]
    live_count = counts[group_index]
    weight = pair_weight[group_index]
    pair_align = align[0]
    all_rows = jnp.arange(pair_rows, dtype=jnp.int32)
    row_live = all_rows < live_count
    perm = target_index(pair_rows, row_count, per_slot, data_size)
    live_pos = (perm[None, :] == pair_align[:, None]) & row_live[:, None]
    col_live = jnp.max(live_pos.astype(jnp.int32), axis=0) > 0
    x_all = ring_gather(src_emb, ring, lang_size)
    y_all = ring_gather(partner, ring, lang_size)

    block = max(1, min(pair_rows, BLOCK_BYTES // (4 * pair_rows)))
    steps = pair_rows // block
    if steps == 1:
        is_pos = perm[None, :] == pair_align[:, None]
        scores_f = scores_of(x_all, y_all, is_pos, inv_root)
        row_lse, pos_score, col_max, col_sum = block_stats(scores_f, is_pos, row_live, col_live)
    else:
        def one_block(k, carry):
            row_lse, pos_score, col_max, col_sum = carry
            start = k * block
            x_blk = lax.dynamic_slice_in_dim(x_all, start, block)
            a_blk = lax.dynamic_slice_in_dim(pair_align, start, block)
            r_blk = lax.dynamic_slice_in_dim(row_live, start, block)
            is_pos = perm[None, :] == a_blk[:, None]
            s_blk = scores_of(x_blk, y_all, is_pos, inv_root)
            b_lse, b_pos, b_max, b_sum = block_stats(s_blk, is_pos, r_blk, col_live)
            top = jnp.maximum(col_max, b_max)
            col_sum = col_sum * jnp.exp(col_max - top) + b_sum * jnp.exp(b_max - top)
            row_lse = lax.dynamic_update_slice_in_dim(row_lse, b_lse, start, 0)
            pos_score = lax.dynamic_update_slice_in_dim(pos_score, b_pos, start, 0)
            return row_lse, pos_score, top, col_sum

        zeros = jnp.zeros((pair_rows,), jnp.float32)
        init = (zeros, zeros, jnp.full((pair_rows,), LOW_FILL, jnp.float32), zeros)
        row_lse, pos_score, col_max, col_sum = lax.fori_loop(0, steps, one_block, init)
    col_lse = col_max + jnp.log(col_sum + (1.0 - col_live.astype(jnp.float32)))

    row_f = row_live.astype(jnp.float32)
    col_f = col_live.astype(jnp.float32)
    total = jnp.sum(row_f * (row_lse - 2.0 * pos_score)) + jnp.sum(col_f * col_lse)
    pair_loss = (total / live_count.astype(jnp.float32)).reshape(1)

    mine = shard_index * row_count
    a_my = lax.dynamic_slice_in_dim(pair_align, mine, row_count)
    r_my = (mine + jnp.arange(row_count, dtype=jnp.int32)) < live_count
    lse_my = lax.dynamic_slice_in_dim(row_lse, mine, row_count)
    pos_rows = perm[None, :] == a_my[:, None]
    if steps == 1:
        s_rows = lax.dynamic_slice_in_dim(scores_f, mine, row_count, 0)
    else:
        s_rows = scores_of(src_emb, y_all, pos_rows, inv_root)
    g_rows = grad_of(s_rows, pos_rows, r_my, col_live, lse_my, col_lse, weight)
    grad_src = (
        jnp.dot(g_rows, y_all, preferred_element_type=jnp.float32) * inv_root
    ).astype(jnp.bfloat16)

    q_my = jnp.arange(row_count, dtype=jnp.int32)
    p_my = (q_my // per_slot * data_size + shard_index) * per_slot + q_my % per_slot
    clse_my = lax.dynamic_slice_in_dim(col_lse, mine, row_count)
    pos_cols = p_my[None, :] == pair_align[:, None]
    c_my = jnp.max((pos_cols & row_live[:, None]).astype(jnp.int32), axis=0) > 0
    if steps == 1:
        s_cols = lax.dynamic_slice_in_dim(scores_f, mine, row_count, 1)
    else:
        s_cols = scores_of(x_all, partner, pos_cols, inv_root)
    g_cols = grad_of(s_cols, pos_cols, row_live, c_my, row_lse, clse_my, weight)
    own_terms = lax.dot_general(
        g_cols, x_all, (((0,), (0,)), ((), ())), preferred_element_type=jnp.float32
    )
    grad_local = (own_terms * inv_root).astype(jnp.bfloat16)
    returned = lax.all_to_all(
        grad_local.reshape(lang_size, per_slot, emb_width), "lang", split_axis=0, concat_axis=0, tiled=True
    )
    choose = (slot_group[:, None] == jnp.arange(lang_size, dtype=jnp.int32)[None, :]).astype(returned.dtype)
    grad_tgt = jnp.einsum(
        "sg,grd->srd", choose, returned, preferred_element_type=jnp.float32
    ).astype(returned.dtype)
    return (grad_src, grad_tgt, pair_loss)


def solution(mesh):
    in_specs = (
        P(("lang", "dp"), None),
        P(None, ("lang", "dp"), None),
        P(),
        P(),
        P("lang", None),
        P(),
    )
    out_specs = (P(("lang", "dp"), None), P(None, ("lang", "dp"), None), P("lang"))
    return jax.shard_map(
        functools.partial(per_device, snake_ring(mesh)), mesh=mesh, in_specs=in_specs, out_specs=out_specs, check_vma=False
    )
```

```python
import functools
import math

import jax
import jax.numpy as jnp
from jax import lax
from jax.sharding import PartitionSpec as P

MARGIN = 0.3
LOW_FILL = -1e30
BLOCK_BYTES = 8 * 1024 * 1024


def target_index(col_count, row_count, per_slot, data_size):
    position = jnp.arange(col_count, dtype=jnp.int32)
    source = position // row_count
    within = position % row_count
    return (within // per_slot * data_size + source) * per_slot + within % per_slot


def snake_ring(mesh):
    count = mesh.shape["dp"]
    try:
        spots = [tuple(dev.coords) for dev in mesh.devices.reshape(-1, count)[0]]
    except (AttributeError, TypeError):
        return list(range(count))
    ys = sorted({s[1] for s in spots})
    zs = sorted({s[2] for s in spots})
    where = {(s[1], s[2]): d for d, s in enumerate(spots)}
    if len(where) != count or len(ys) * len(zs) != count:
        return list(range(count))
    rows, cols = (ys, zs) if len(ys) % 2 == 0 else (zs, ys)
    at = lambda r, c: where[(r, c) if rows is ys else (c, r)]
    if len(rows) == 1 or len(cols) == 1:
        return [at(r, c) for r in rows for c in cols]
    order = [at(rows[0], cols[0])]
    for k, r in enumerate(rows):
        seq = cols[1:] if k % 2 == 0 else cols[:0:-1]
        order += [at(r, c) for c in seq]
    order += [at(r, cols[0]) for r in rows[:0:-1]]
    return order


def ring_gather(block, ring, lang_size):
    count = len(ring)
    place = [0] * count
    for p, d in enumerate(ring):
        place[d] = p
    ring_arr = jnp.array(ring, jnp.int32)
    my_dp = lax.axis_index("dp")
    my_pos = jnp.array(place, jnp.int32)[my_dp]
    mirror = 1 - 2 * (lax.axis_index("lang") % 2)

    def pairs_for(even_step):
        out = []
        for l in range(lang_size):
            step = even_step if l % 2 == 0 else -even_step
            out += [(l * count + ring[p], l * count + ring[(p + step) % count]) for p in range(count)]
        return out

    rows = block.shape[0]
    out = jnp.zeros((count * rows,) + block.shape[1:], block.dtype)
    out = lax.dynamic_update_slice_in_dim(out, block, my_dp * rows, 0)
    for even_step, steps in ((1, count // 2), (-1, count - 1 - count // 2)):
        pairs = pairs_for(even_step)
        cur = block
        for t in range(1, steps + 1):
            cur = lax.ppermute(cur, ("lang", "dp"), pairs)
            origin = ring_arr[(my_pos - even_step * mirror * t) % count]
            out = lax.dynamic_update_slice_in_dim(out, cur, origin * rows, 0)
    return out


def scores_of(x_rows, y_rows, pos_mask, inv_root):
    raw_dot = lax.dot_general(
        x_rows, y_rows, (((1,), (1,)), ((), ())), preferred_element_type=jnp.float32
    )
    return raw_dot * inv_root - MARGIN * pos_mask.astype(jnp.float32)


def block_stats(scores_f, is_pos, row_live, col_ok):
    row_max = jnp.max(jnp.where(col_ok[None, :], scores_f, LOW_FILL), axis=1)
    row_sum = jnp.sum(
        jnp.where(col_ok[None, :], jnp.exp(scores_f - row_max[:, None]), 0.0), axis=1
    )
    row_lse = row_max + jnp.log(row_sum + (1.0 - row_live.astype(jnp.float32)))
    pos_score = jnp.sum(jnp.where(is_pos, scores_f, 0.0), axis=1)
    col_max = jnp.max(jnp.where(row_live[:, None], scores_f, LOW_FILL), axis=0)
    col_sum = jnp.sum(
        jnp.where(row_live[:, None], jnp.exp(scores_f - col_max[None, :]), 0.0), axis=0
    )
    return row_lse, pos_score, col_max, col_sum


def grad_of(scores_f, is_pos, row_ok, col_ok, row_lse, col_lse, weight):
    both_live = row_ok[:, None] & col_ok[None, :]
    by_row = jnp.where(both_live, jnp.exp(scores_f - row_lse[:, None]), 0.0)
    by_col = jnp.where(both_live, jnp.exp(scores_f - col_lse[None, :]), 0.0)
    pos_hit = (is_pos & row_ok[:, None]).astype(jnp.float32)
    return (weight * (by_row + by_col - 2.0 * pos_hit)).astype(jnp.bfloat16)


def per_device(ring, src_emb, tgt_emb, slot_group, counts, align, pair_weight):
    lang_size = lax.axis_size("lang")
    data_size = lax.axis_size("dp")
    row_count, emb_width = src_emb.shape
    per_slot = tgt_emb.shape[1]
    pair_rows = row_count * data_size
    inv_root = 1.0 / math.sqrt(emb_width)
    group_index = lax.axis_index("lang")
    shard_index = lax.axis_index("dp")
    slot_ids = jnp.arange(lang_size, dtype=jnp.int32)
    slot_of_group = jnp.zeros((lang_size,), jnp.int32).at[slot_group].set(slot_ids)
    ordered = tgt_emb[slot_of_group]
    arrived = lax.all_to_all(ordered, "lang", split_axis=0, concat_axis=1, tiled=True)
    partner = arrived[0]
    live_count = counts[group_index]
    weight = pair_weight[group_index]
    pair_align = align[0]
    all_rows = jnp.arange(pair_rows, dtype=jnp.int32)
    row_live = all_rows < live_count
    perm = target_index(pair_rows, row_count, per_slot, data_size)
    live_pos = (perm[None, :] == pair_align[:, None]) & row_live[:, None]
    col_live = jnp.max(live_pos.astype(jnp.int32), axis=0) > 0
    x_all = ring_gather(src_emb, ring, lang_size)
    y_all = ring_gather(partner, ring, lang_size)

    block = max(1, min(pair_rows, BLOCK_BYTES // (4 * pair_rows)))
    steps = pair_rows // block
    if steps == 1:
        is_pos = perm[None, :] == pair_align[:, None]
        scores_f = scores_of(x_all, y_all, is_pos, inv_root)
        row_lse, pos_score, col_max, col_sum = block_stats(scores_f, is_pos, row_live, col_live)
    else:
        def one_block(k, carry):
            row_lse, pos_score, col_max, col_sum = carry
            start = k * block
            x_blk = lax.dynamic_slice_in_dim(x_all, start, block)
            a_blk = lax.dynamic_slice_in_dim(pair_align, start, block)
            r_blk = lax.dynamic_slice_in_dim(row_live, start, block)
            is_pos = perm[None, :] == a_blk[:, None]
            s_blk = scores_of(x_blk, y_all, is_pos, inv_root)
            b_lse, b_pos, b_max, b_sum = block_stats(s_blk, is_pos, r_blk, col_live)
            top = jnp.maximum(col_max, b_max)
            col_sum = col_sum * jnp.exp(col_max - top) + b_sum * jnp.exp(b_max - top)
            row_lse = lax.dynamic_update_slice_in_dim(row_lse, b_lse, start, 0)
            pos_score = lax.dynamic_update_slice_in_dim(pos_score, b_pos, start, 0)
            return row_lse, pos_score, top, col_sum

        zeros = jnp.zeros((pair_rows,), jnp.float32)
        init = (zeros, zeros, jnp.full((pair_rows,), LOW_FILL, jnp.float32), zeros)
        row_lse, pos_score, col_max, col_sum = lax.fori_loop(0, steps, one_block, init)
    col_lse = col_max + jnp.log(col_sum + (1.0 - col_live.astype(jnp.float32)))

    row_f = row_live.astype(jnp.float32)
    col_f = col_live.astype(jnp.float32)
    total = jnp.sum(row_f * (row_lse - 2.0 * pos_score)) + jnp.sum(col_f * col_lse)
    pair_loss = (total / live_count.astype(jnp.float32)).reshape(1)

    mine = shard_index * row_count
    a_my = lax.dynamic_slice_in_dim(pair_align, mine, row_count)
    r_my = (mine + jnp.arange(row_count, dtype=jnp.int32)) < live_count
    lse_my = lax.dynamic_slice_in_dim(row_lse, mine, row_count)
    if steps == 1:
        pos_rows = lax.dynamic_slice_in_dim(is_pos, mine, row_count, 0)
    else:
        pos_rows = perm[None, :] == a_my[:, None]
    if steps == 1:
        s_rows = lax.dynamic_slice_in_dim(scores_f, mine, row_count, 0)
    else:
        s_rows = scores_of(src_emb, y_all, pos_rows, inv_root)
    g_rows = grad_of(s_rows, pos_rows, r_my, col_live, lse_my, col_lse, weight)
    grad_src = (
        jnp.dot(g_rows, y_all, preferred_element_type=jnp.float32) * inv_root
    ).astype(jnp.bfloat16)

    q_my = jnp.arange(row_count, dtype=jnp.int32)
    p_my = (q_my // per_slot * data_size + shard_index) * per_slot + q_my % per_slot
    clse_my = lax.dynamic_slice_in_dim(col_lse, mine, row_count)
    if steps == 1:
        pos_cols = lax.dynamic_slice_in_dim(is_pos, mine, row_count, 1)
    else:
        pos_cols = p_my[None, :] == pair_align[:, None]
    c_my = jnp.max((pos_cols & row_live[:, None]).astype(jnp.int32), axis=0) > 0
    if steps == 1:
        s_cols = lax.dynamic_slice_in_dim(scores_f, mine, row_count, 1)
    else:
        s_cols = scores_of(x_all, partner, pos_cols, inv_root)
    g_cols = grad_of(s_cols, pos_cols, row_live, c_my, row_lse, clse_my, weight)
    own_terms = lax.dot_general(
        g_cols, x_all, (((0,), (0,)), ((), ())), preferred_element_type=jnp.float32
    )
    grad_local = (own_terms * inv_root).astype(jnp.bfloat16)
    returned = lax.all_to_all(
        grad_local.reshape(lang_size, per_slot, emb_width), "lang", split_axis=0, concat_axis=0, tiled=True
    )
    choose = (slot_group[:, None] == jnp.arange(lang_size, dtype=jnp.int32)[None, :]).astype(returned.dtype)
    grad_tgt = jnp.einsum(
        "sg,grd->srd", choose, returned, preferred_element_type=jnp.float32
    ).astype(returned.dtype)
    return (grad_src, grad_tgt, pair_loss)


def solution(mesh):
    in_specs = (
        P(("lang", "dp"), None),
        P(None, ("lang", "dp"), None),
        P(),
        P(),
        P("lang", None),
        P(),
    )
    out_specs = (P(("lang", "dp"), None), P(None, ("lang", "dp"), None), P("lang"))
    return jax.shard_map(
        functools.partial(per_device, snake_ring(mesh)), mesh=mesh, in_specs=in_specs, out_specs=out_specs, check_vma=False
    )
```
